128 devices in a mesh: section: 4 (over x), expert: 32 (over y, z, core).
Axes of the slice: x: 4, y: 4, z: 4, core: 2. Of those that a mesh axis runs over, the one named last changes fastest.
Arguments:
- inputs: bfloat16 [2, 256, 2048], P(None, 'expert'), may hold values from -6 to 6
- route_ids: int32 [4, 2, 256, 8], P('section', None, 'expert'), may hold values from 0 to 31, all different within a row; in each aligned block of 8 rows (0 to 7, 8 to 15, ..., all dimensions but the last counted through in order) at most 4 rows name the same one
- route_gates: float32 [4, 2, 256, 8], P('section', None, 'expert'), may hold values from 0.1 to 1
- w_gate: bfloat16 [4, 32, 2048, 768], P('section', 'expert'), may hold values from -0.125 to 0.125
- w_up: bfloat16 [4, 32, 2048, 768], P('section', 'expert'), may hold values from -0.125 to 0.125
- w_down: bfloat16 [4, 32, 768, 2048], P('section', 'expert'), may hold values from -0.21875 to 0.21875
- cotangent: bfloat16 [2, 256, 2048], P(None, 'expert'), may hold values from -6 to 6
Outputs:
- section_out: bfloat16 [4, 2, 256, 2048], P('section', None, 'expert')
- grad_input: bfloat16 [4, 2, 256, 2048], P('section', None, 'expert')
- grad_gates: float32 [4, 2, 256, 8], P('section', None, 'expert')
- grad_w_gate: bfloat16 [4, 32, 2048, 768], P('section', 'expert')
- grad_w_up: bfloat16 [4, 32, 2048, 768], P('section', 'expert')
- grad_w_down: bfloat16 [4, 32, 768, 2048], P('section', 'expert')
The draws below stay inside these ranges and needn't reach their ends.
Inputs may be any that keep to these rules, and one draw needn't show every extreme that they name: `route_ids`: A token's 8 ids differ. In each layer and micro-batch, the 8 tokens of one device name no expert more than 4 times, a bound that some block reaches; every expert is named somewhere.
All inputs are finite; a program needn't handle non-finite values.
Results may differ from the reference program's by a relative error of at most 0.023.
Values may be sent and summed in bfloat16 or wider, within the bound.
No kernel may reach another device: no remote copies, remote signals or barrier semaphores. Data moves between devices by JAX's collectives and lax.ppermute only.
A program may use at most 128 MiB of HBM per device.

```python
import math
import jax
import jax.numpy as jnp
import numpy as np
from jax import lax

D = 2048
FF = 768
TOP = 8
MB = 2
TOK_MB = 8
SECTIONS = 4
EXPERTS = 32
TOKENS = 256
MOST = 4
N_EXPERT = 32


def shard_levels(stream_key, dims, split, smallest, largest):
    def one(axis_at, blocks):
        draws = jax.random.uniform(jax.random.fold_in(jax.random.fold_in(stream_key, 6), axis_at), (blocks,), jnp.float32, smallest / len(split), largest / len(split))
        return jnp.repeat(jnp.exp(draws), dims[axis_at] // blocks).reshape((-1,) + (1,) * (len(dims) - axis_at - 1))

    gain = one(*split[0])
    for cut in split[1:]:
        gain = gain * one(*cut)
    return gain


def routed_block(own_key, own, number, rows, amount, top, most, slope):
    ranking = jax.random.permutation(own_key, amount)
    packed, usual = shares(amount, rows * top, most, slope, True), shares(amount, rows * top, most, slope, False)
    places = jnp.arange(amount)

    def named(tallies, offset_by):
        used = int((tallies > 0).sum())
        fixed = max(1, used // 4)
        moved = fixed + (places - fixed + offset_by * (used - fixed)) % max(1, amount - fixed)
        return jnp.zeros((amount,), jnp.int32).at[ranking[jnp.where(places < fixed, places, moved)]].set(jnp.asarray(tallies, jnp.int32))

    tallies = jnp.where(number % 4 == 0, named(packed, number // 4), named(usual, number - number // 4 - 1))
    mixed = jax.random.permutation(jax.random.fold_in(own, 3), amount)
    donor, sink = mixed[0:amount // 2 * 2:2], mixed[1:amount // 2 * 2:2]
    margin = jnp.minimum(tallies[donor] - 1, most - tallies[sink]) // 2
    margin = jnp.where((donor == ranking[0]) | (sink == ranking[0]) | (tallies[sink] == 0), 0, jnp.maximum(margin, 0))
    moved = jax.random.randint(jax.random.fold_in(own, 4), (amount // 2,), 0, 1 << 20) % (margin + 1)
    tallies = tallies.at[donor].add(-moved).at[sink].add(moved)
    items = jnp.searchsorted(jnp.cumsum(tallies), jnp.arange(rows * top), side="right").astype(jnp.int32)
    grid = items.reshape(top, rows).T
    grid = grid[jax.random.permutation(jax.random.fold_in(own, 1), rows)]
    offset_by = jax.random.randint(jax.random.fold_in(own, 2), (rows, 1), 0, top)
    return jnp.take_along_axis(grid, (jnp.arange(top)[None, :] + offset_by) % top, axis=1)


def shares(number_of, total, most, lean, full):
    weights = [(1 << 20) // math.isqrt(grade ** lean) + 1 for grade in range(1, number_of + 1)]
    largest = most if full else min(most, max(-(-total // number_of), total * weights[0] // sum(weights)))
    least = 1 if total - largest >= number_of - 1 else 0
    holding, surplus = [largest] + [least] * (number_of - 1), total - largest - least * (number_of - 1)
    while surplus > 0:
        candidates = [i for i in range(1, number_of) if holding[i] < largest] or [i for i in range(1, number_of) if holding[i] < most]
        whole, remaining = sum([weights[i] for i in candidates]), surplus
        for i in candidates:
            extra = min(most - holding[i], max(1, remaining * weights[i] // whole), surplus)
            holding[i] = holding[i] + extra
            surplus = surplus - extra
    return np.array(holding)


def scatter_about(stream_key, extent, width, bound, cuts=(), kind=jnp.bfloat16):
    drawn = jax.random.normal(stream_key, extent, jnp.float32) * width
    if len(cuts) > 0:
        drawn = shard_levels(stream_key, extent, cuts, -0.22, 0.18) * drawn
    return jnp.clip(drawn, min=-bound, max=bound).astype(kind)


def setup_inputs(seed: int = 0) -> dict:
    key_list = jax.random.split(jax.random.key(seed), 8)
    inputs = scatter_about(key_list[0], (MB, TOKENS, D), 1.0, 6.0, ((1, 32),))
    route_ids_keys = jax.random.split(jax.random.fold_in(key_list[1], 1), SECTIONS * MB * TOKENS // TOK_MB)
    route_ids_turns = jax.random.permutation(jax.random.fold_in(key_list[1], 3), SECTIONS * MB * TOKENS // TOK_MB)
    route_ids = jax.vmap(lambda own, number: routed_block(jax.random.fold_in(key_list[1], 2), own, number, TOK_MB, EXPERTS, TOP, MOST, 2))(route_ids_keys, route_ids_turns).reshape((SECTIONS, MB, TOKENS, TOP))
    route_gates = jnp.clip(jnp.exp(math.log(1.0) - 2.3025851 * jax.random.uniform(key_list[2], (SECTIONS, MB, TOKENS, TOP), jnp.float32) ** shard_levels(key_list[2], (SECTIONS, MB, TOKENS, TOP), ((0, 4), (2, 32)), -0.2, 0.2)), 0.1, 1.0)
    w_gate = scatter_about(key_list[3], (SECTIONS, EXPERTS, D, FF), D ** -0.5, 0.125, ((0, 4), (1, 32)))
    w_up = scatter_about(key_list[4], (SECTIONS, EXPERTS, D, FF), D ** -0.5, 0.125, ((0, 4), (1, 32)))
    w_down = scatter_about(key_list[5], (SECTIONS, EXPERTS, FF, D), FF ** -0.5, 0.21875, ((0, 4), (1, 32)))
    cotangent = scatter_about(key_list[6], (MB, TOKENS, D), 1.0, 6.0, ((1, 32),))
    return dict(inputs=inputs, route_ids=route_ids, route_gates=route_gates, w_gate=w_gate, w_up=w_up, w_down=w_down, cotangent=cotangent)


EPS = 1e-06

def route_slots(flat_ids, capacity):
    expert_ids = jnp.arange(EXPERTS, dtype=jnp.int32)
    onehot = (flat_ids[:, None] == expert_ids[None, :]).astype(jnp.int32)
    ranks = (jnp.cumsum(onehot, axis=0) - onehot).astype(jnp.int32)
    position = lax.optimization_barrier(jnp.sum(ranks * onehot, axis=1)).astype(jnp.int32)
    return (flat_ids * capacity + position).astype(jnp.int32)

def expert_forward(row_data, gate_mat, up_mat, down_mat):
    gate_pre = jnp.dot(row_data, gate_mat, preferred_element_type=jnp.float32)
    up_pre = jnp.dot(row_data, up_mat, preferred_element_type=jnp.float32)
    hidden = (gate_pre * jax.nn.sigmoid(gate_pre) * up_pre).astype(jnp.bfloat16)
    return jnp.dot(hidden, down_mat, preferred_element_type=jnp.float32).astype(jnp.bfloat16)

def expert_backward(row_data, grad_rows, gate_mat, up_mat, down_mat):
    gate_pre = jnp.dot(row_data, gate_mat, preferred_element_type=jnp.float32)
    up_pre = jnp.dot(row_data, up_mat, preferred_element_type=jnp.float32)
    sigma = jax.nn.sigmoid(gate_pre)
    active = gate_pre * sigma
    hidden = (active * up_pre).astype(jnp.bfloat16)
    grad_hidden = jnp.dot(grad_rows, down_mat.T, preferred_element_type=jnp.float32)
    grad_down = jnp.dot(hidden.T, grad_rows, preferred_element_type=jnp.float32)
    grad_gate_pre = (grad_hidden * up_pre * sigma * (1.0 + gate_pre * (1.0 - sigma))).astype(jnp.bfloat16)
    grad_up_pre = (grad_hidden * active).astype(jnp.bfloat16)
    grad_gate = jnp.dot(row_data.T, grad_gate_pre, preferred_element_type=jnp.float32)
    grad_up = jnp.dot(row_data.T, grad_up_pre, preferred_element_type=jnp.float32)
    grad_back = jnp.dot(grad_gate_pre, gate_mat.T, preferred_element_type=jnp.float32) + jnp.dot(grad_up_pre, up_mat.T, preferred_element_type=jnp.float32)
    return (grad_back.astype(jnp.bfloat16), grad_gate, grad_up, grad_down)

def layer_forward(layer_in, ids_now, gates_now, gate_all, up_all, down_all):
    capacity = N_EXPERT * MOST
    x_float = layer_in.astype(jnp.float32)
    scale = lax.rsqrt(lax.optimization_barrier(jnp.mean(x_float * x_float, axis=-1, keepdims=True)) + EPS)
    normed = (x_float * scale).astype(jnp.bfloat16)
    slot_index = route_slots(ids_now.reshape(-1).astype(jnp.int32), capacity)
    row_data = jnp.repeat(normed, TOP, axis=0)
    buffer = jnp.zeros((EXPERTS * capacity, D), jnp.bfloat16).at[slot_index].set(row_data)
    buffer = buffer.reshape(EXPERTS, capacity, D)
    results = lax.map(lambda items: expert_forward(items[0], items[1], items[2], items[3]), (buffer, gate_all, up_all, down_all))
    gathered = results.reshape(-1, D)[slot_index].reshape(TOKENS, TOP, D)
    mixed = x_float + lax.optimization_barrier(jnp.sum(gates_now[:, :, None] * gathered.astype(jnp.float32), axis=1))
    return (mixed.astype(jnp.bfloat16), buffer, gathered, slot_index, x_float, scale)

def layer_backward(layer_in, grad_out, ids_now, gates_now, gate_all, up_all, down_all):
    capacity = N_EXPERT * MOST
    mixed, buffer, gathered, slot_index, x_float, scale = layer_forward(layer_in, ids_now, gates_now, gate_all, up_all, down_all)
    grad_float = grad_out.astype(jnp.float32)
    grad_mix = lax.optimization_barrier(jnp.sum(grad_float[:, None, :] * gathered.astype(jnp.float32), axis=-1))
    grad_rows = (gates_now[:, :, None] * grad_float[:, None, :]).astype(jnp.bfloat16).reshape(-1, D)
    grad_buffer = jnp.zeros((EXPERTS * capacity, D), jnp.bfloat16).at[slot_index].set(grad_rows)
    grad_buffer = grad_buffer.reshape(EXPERTS, capacity, D)
    grad_back, grad_gate, grad_up, grad_down = lax.map(lambda items: expert_backward(items[0], items[1], items[2], items[3], items[4]), (buffer, grad_buffer, gate_all, up_all, down_all))
    grad_norm = lax.optimization_barrier(jnp.sum(grad_back.reshape(-1, D)[slot_index].reshape(TOKENS, TOP, D).astype(jnp.float32), axis=1))
    inner = lax.optimization_barrier(jnp.mean(grad_norm * x_float, axis=-1, keepdims=True))
    grad_in = grad_float + scale * grad_norm - x_float * (scale * scale * scale) * inner
    return (grad_in.astype(jnp.bfloat16), grad_mix, grad_gate, grad_up, grad_down)

def reference(inputs, route_ids, route_gates, w_gate, w_up, w_down, cotangent):
    layer_inputs = []
    layer_outputs = []
    for section_number in range(SECTIONS):
        ins_here = []
        outs_here = []
        for batch_number in range(MB):
            if section_number == 0:
                layer_in = inputs[batch_number]
            else:
                layer_in = layer_outputs[section_number - 1][batch_number]
            mixed = layer_forward(layer_in, route_ids[section_number, batch_number], route_gates[section_number, batch_number], w_gate[section_number], w_up[section_number], w_down[section_number])[0]
            ins_here.append(layer_in)
            outs_here.append(mixed)
        layer_inputs.append(ins_here)
        layer_outputs.append(outs_here)
    grad_inputs = [None] * SECTIONS
    grad_mixes = [None] * SECTIONS
    gate_grads = [None] * SECTIONS
    up_grads = [None] * SECTIONS
    down_grads = [None] * SECTIONS
    for section_number in reversed(range(SECTIONS)):
        ins_grad = []
        mix_grad = []
        gate_sum = jnp.zeros((EXPERTS, D, FF), jnp.float32)
        up_sum = jnp.zeros((EXPERTS, D, FF), jnp.float32)
        down_sum = jnp.zeros((EXPERTS, FF, D), jnp.float32)
        for batch_number in range(MB):
            if section_number == SECTIONS - 1:
                grad_out = cotangent[batch_number]
            else:
                grad_out = grad_inputs[section_number + 1][batch_number]
            grad_in, grad_mix, grad_gate, grad_up, grad_down = layer_backward(layer_inputs[section_number][batch_number], grad_out, route_ids[section_number, batch_number], route_gates[section_number, batch_number], w_gate[section_number], w_up[section_number], w_down[section_number])
            ins_grad.append(grad_in)
            mix_grad.append(grad_mix)
            gate_sum = gate_sum + grad_gate
            up_sum = up_sum + grad_up
            down_sum = down_sum + grad_down
        grad_inputs[section_number] = ins_grad
        grad_mixes[section_number] = mix_grad
        gate_grads[section_number] = gate_sum.astype(jnp.bfloat16)
        up_grads[section_number] = up_sum.astype(jnp.bfloat16)
        down_grads[section_number] = down_sum.astype(jnp.bfloat16)
    section_out = jnp.stack([jnp.stack(item) for item in layer_outputs])
    grad_input = jnp.stack([jnp.stack(item) for item in grad_inputs])
    grad_gates = jnp.stack([jnp.stack(item) for item in grad_mixes])
    return (section_out, grad_input, grad_gates, jnp.stack(gate_grads), jnp.stack(up_grads), jnp.stack(down_grads))
```

```python
import jax
import jax.numpy as jnp
from jax import lax
from jax.sharding import PartitionSpec as P

EPS = 1e-06


def hop(value, axis, source, target):
    return lax.ppermute(value, axis, [(source, target)])


def slot_matrices(ids, expert_count, most):
    micro_count, tok_count, top_count = ids.shape
    per_mb = tok_count * top_count
    flat = ids.reshape(micro_count, per_mb)
    order = jnp.arange(per_mb)
    earlier = order[:, None] > order[None, :]
    same = flat[:, :, None] == flat[:, None, :]
    position = jnp.sum(same & earlier[None], axis=2).astype(jnp.int32)
    micro = jnp.arange(micro_count, dtype=jnp.int32)[:, None]
    slot = flat * (micro_count * most) + micro * most + position
    slot = slot.reshape(-1)
    total_slots = expert_count * micro_count * most
    rows_mat = (jnp.arange(total_slots, dtype=jnp.int32)[:, None] == slot[None, :]).astype(jnp.bfloat16)
    tok_mat = rows_mat.reshape(total_slots, micro_count * tok_count, top_count).sum(axis=2)
    return rows_mat, tok_mat.astype(jnp.bfloat16)


def all_to_all(buffer, devices, width):
    shaped = buffer.reshape(devices, -1, width)
    out = lax.all_to_all(shaped, "expert", split_axis=0, concat_axis=0, tiled=True)
    return out.reshape(-1, width)


def body(inputs, route_ids, route_gates, w_gate, w_up, w_down, cotangent):
    section_count = lax.axis_size("section")
    section_index = lax.axis_index("section")
    devices = lax.axis_size("expert")
    micro_count, tok_count, width = inputs.shape
    top_count = route_ids.shape[3]
    exp_dev = w_gate.shape[1]
    hidden_width = w_gate.shape[3]
    expert_count = exp_dev * devices
    most = min(tok_count, 2 * tok_count * top_count // expert_count)
    slots_per = micro_count * most
    tokens = micro_count * tok_count
    gate_mat, up_mat, down_mat = (w_gate[0], w_up[0], w_down[0])
    ids = route_ids[0]
    gates = route_gates[0].reshape(tokens, top_count)
    rows_mat, tok_mat = slot_matrices(ids, expert_count, most)

    def to_experts(rows):
        return rows.reshape(devices, exp_dev, slots_per, -1)

    def forward_step(layer_in):
        x_float = layer_in.astype(jnp.float32)
        scale = lax.rsqrt(jnp.mean(x_float * x_float, axis=-1, keepdims=True) + EPS)
        normed = (x_float * scale).astype(jnp.bfloat16)
        buffer = jnp.dot(tok_mat, normed, preferred_element_type=jnp.float32).astype(jnp.bfloat16)
        received = to_experts(all_to_all(buffer, devices, width))
        gate_pre = jnp.einsum("nemd,edf->nemf", received, gate_mat, preferred_element_type=jnp.float32)
        up_pre = jnp.einsum("nemd,edf->nemf", received, up_mat, preferred_element_type=jnp.float32)
        hidden = (gate_pre * jax.nn.sigmoid(gate_pre) * up_pre).astype(jnp.bfloat16)
        results = jnp.einsum(
            "nemf,efd->nemd", hidden, down_mat, preferred_element_type=jnp.float32
        ).astype(jnp.bfloat16)
        returned = all_to_all(results.reshape(-1, width), devices, width)
        gathered = jnp.dot(rows_mat.T, returned, preferred_element_type=jnp.float32).astype(jnp.bfloat16)
        gathered = gathered.reshape(tokens, top_count, width)
        mixed = x_float + jnp.sum(gates[:, :, None] * gathered.astype(jnp.float32), axis=1)
        saved = (x_float, scale, received, gate_pre, up_pre, hidden, gathered)
        return mixed.astype(jnp.bfloat16), saved

    def backward_step(grad_out, saved):
        x_float, scale, received, gate_pre, up_pre, hidden, gathered = saved
        grad_float = grad_out.astype(jnp.float32)
        grad_mix = jnp.sum(grad_float[:, None, :] * gathered.astype(jnp.float32), axis=-1)
        grad_rows = (gates[:, :, None] * grad_float[:, None, :]).astype(jnp.bfloat16).reshape(-1, width)
        gbuf = jnp.dot(rows_mat, grad_rows, preferred_element_type=jnp.float32).astype(jnp.bfloat16)
        grad_received = to_experts(all_to_all(gbuf, devices, width))
        sigma = jax.nn.sigmoid(gate_pre)
        active = gate_pre * sigma
        grad_hidden = jnp.einsum(
            "nemd,efd->nemf", grad_received, down_mat, preferred_element_type=jnp.float32
        )
        grad_gate_pre = (grad_hidden * up_pre * sigma * (1.0 + gate_pre * (1.0 - sigma))).astype(
            jnp.bfloat16
        )
        grad_up_pre = (grad_hidden * active).astype(jnp.bfloat16)
        grad_back = (
            jnp.einsum("nemf,edf->nemd", grad_gate_pre, gate_mat, preferred_element_type=jnp.float32)
            + jnp.einsum("nemf,edf->nemd", grad_up_pre, up_mat, preferred_element_type=jnp.float32)
        ).astype(jnp.bfloat16)
        returned = all_to_all(grad_back.reshape(-1, width), devices, width)
        grad_norm = jnp.dot(tok_mat.T, returned, preferred_element_type=jnp.float32)
        inner = jnp.mean(grad_norm * x_float, axis=-1, keepdims=True)
        grad_in = grad_float + scale * grad_norm - x_float * (scale * scale * scale) * inner
        kept = (received, grad_received, grad_gate_pre, grad_up_pre, hidden)
        return grad_in.astype(jnp.bfloat16), grad_mix, kept

    layer_in = inputs.reshape(tokens, width)
    outs = []
    saves = []
    for step in range(section_count):
        if step > 0:
            layer_in = hop(outs[-1], "section", step - 1, step)
        mixed, saved = forward_step(layer_in)
        outs.append(mixed)
        saves.append(saved)
    grad_out = cotangent.reshape(tokens, width)
    grads_in = [None] * section_count
    mixes = [None] * section_count
    kepts = [None] * section_count
    for step in reversed(range(section_count)):
        if step < section_count - 1:
            grad_out = hop(grads_in[step + 1], "section", step + 1, step)
        grads_in[step], mixes[step], kepts[step] = backward_step(grad_out, saves[step])

    def pick(values):
        result = values[0]
        for step in range(1, section_count):
            result = jnp.where(section_index == step, values[step], result)
        return result

    def weight_grads(kept):
        received, grad_received, grad_gate_pre, grad_up_pre, hidden = kept
        grad_gate = jnp.einsum(
            "nemd,nemf->edf", received, grad_gate_pre, preferred_element_type=jnp.float32
        )
        grad_up = jnp.einsum("nemd,nemf->edf", received, grad_up_pre, preferred_element_type=jnp.float32)
        grad_down = jnp.einsum(
            "nemf,nemd->efd", hidden, grad_received, preferred_element_type=jnp.float32
        )
        return (
            grad_gate.astype(jnp.bfloat16),
            grad_up.astype(jnp.bfloat16),
            grad_down.astype(jnp.bfloat16),
        )

    branches = [lambda k=k: weight_grads(kepts[k]) for k in range(section_count)]
    grad_gate, grad_up, grad_down = lax.switch(section_index, branches)
    section_out = pick(outs).reshape(1, micro_count, tok_count, width)
    grad_input = pick(grads_in).reshape(1, micro_count, tok_count, width)
    grad_gates = pick(mixes).reshape(1, micro_count, tok_count, top_count)
    return (
        section_out,
        grad_input,
        grad_gates,
        grad_gate[None],
        grad_up[None],
        grad_down[None],
    )


def solution(mesh):
    in_specs = (
        P(None, "expert", None),
        P("section", None, "expert", None),
        P("section", None, "expert", None),
        P("section", "expert", None, None),
        P("section", "expert", None, None),
        P("section", "expert", None, None),
        P(None, "expert", None),
    )
    out_specs = (
        P("section", None, "expert", None),
        P("section", None, "expert", None),
        P("section", None, "expert", None),
        P("section", "expert", None, None),
        P("section", "expert", None, None),
        P("section", "expert", None, None),
    )
    return jax.shard_map(body, mesh=mesh, in_specs=in_specs, out_specs=out_specs, check_vma=False)
```

```python
import jax
import jax.numpy as jnp
from jax import lax
from jax.sharding import PartitionSpec as P

EPS = 1e-06


def hop(value, axis, source, target):
    return lax.ppermute(value, axis, [(source, target)])


def slot_matrices(ids, expert_count, most):
    micro_count, tok_count, top_count = ids.shape
    per_mb = tok_count * top_count
    flat = ids.reshape(micro_count, per_mb)
    order = jnp.arange(per_mb)
    earlier = order[:, None] > order[None, :]
    same = flat[:, :, None] == flat[:, None, :]
    position = jnp.sum(same & earlier[None], axis=2).astype(jnp.int32)
    micro = jnp.arange(micro_count, dtype=jnp.int32)[:, None]
    slot = flat * (micro_count * most) + micro * most + position
    slot = slot.reshape(-1)
    total_slots = expert_count * micro_count * most
    rows_mat = (jnp.arange(total_slots, dtype=jnp.int32)[:, None] == slot[None, :]).astype(jnp.bfloat16)
    tok_mat = rows_mat.reshape(total_slots, micro_count * tok_count, top_count).sum(axis=2)
    return rows_mat, tok_mat.astype(jnp.bfloat16)


def all_to_all(buffer, devices, width):
    shaped = buffer.reshape(devices, -1, width)
    out = lax.all_to_all(shaped, "expert", split_axis=0, concat_axis=0, tiled=True)
    return out.reshape(-1, width)


def body(inputs, route_ids, route_gates, w_gate, w_up, w_down, cotangent):
    section_count = lax.axis_size("section")
    section_index = lax.axis_index("section")
    devices = lax.axis_size("expert")
    micro_count, tok_count, width = inputs.shape
    top_count = route_ids.shape[3]
    exp_dev = w_gate.shape[1]
    hidden_width = w_gate.shape[3]
    expert_count = exp_dev * devices
    most = min(tok_count, 2 * tok_count * top_count // expert_count)
    slots_per = micro_count * most
    tokens = micro_count * tok_count
    gate_mat, up_mat, down_mat = (w_gate[0], w_up[0], w_down[0])
    ids = route_ids[0]
    gates = route_gates[0].reshape(tokens, top_count)
    rows_mat, tok_mat = slot_matrices(ids, expert_count, most)

    def to_experts(rows):
        return rows.reshape(devices, exp_dev, slots_per, -1)

    def expert_forward(received):
        gate_pre = jnp.einsum("nemd,edf->nemf", received, gate_mat, preferred_element_type=jnp.float32)
        up_pre = jnp.einsum("nemd,edf->nemf", received, up_mat, preferred_element_type=jnp.float32)
        hidden = (gate_pre * jax.nn.sigmoid(gate_pre) * up_pre).astype(jnp.bfloat16)
        results = jnp.einsum(
            "nemf,efd->nemd", hidden, down_mat, preferred_element_type=jnp.float32
        ).astype(jnp.bfloat16)
        return gate_pre, up_pre, hidden, results

    def expert_backward(grad_received, gate_pre, up_pre):
        sigma = jax.nn.sigmoid(gate_pre)
        active = gate_pre * sigma
        grad_hidden = jnp.einsum(
            "nemd,efd->nemf", grad_received, down_mat, preferred_element_type=jnp.float32
        )
        grad_gate_pre = (grad_hidden * up_pre * sigma * (1.0 + gate_pre * (1.0 - sigma))).astype(
            jnp.bfloat16
        )
        grad_up_pre = (grad_hidden * active).astype(jnp.bfloat16)
        grad_back = (
            jnp.einsum("nemf,edf->nemd", grad_gate_pre, gate_mat, preferred_element_type=jnp.float32)
            + jnp.einsum("nemf,edf->nemd", grad_up_pre, up_mat, preferred_element_type=jnp.float32)
        ).astype(jnp.bfloat16)
        return grad_back, grad_gate_pre, grad_up_pre

    def grad_buffer(grad_float):
        grad_rows = (gates[:, :, None] * grad_float[:, None, :]).astype(jnp.bfloat16).reshape(-1, width)
        return jnp.dot(rows_mat, grad_rows, preferred_element_type=jnp.float32).astype(jnp.bfloat16)

    def token_forward(x_float, returned):
        gathered = jnp.dot(rows_mat.T, returned, preferred_element_type=jnp.float32).astype(jnp.bfloat16)
        gathered = gathered.reshape(tokens, top_count, width)
        mixed = x_float + jnp.sum(gates[:, :, None] * gathered.astype(jnp.float32), axis=1)
        return mixed.astype(jnp.bfloat16), gathered

    def token_backward(grad_float, x_float, scale, gathered, returned):
        grad_mix = jnp.sum(grad_float[:, None, :] * gathered.astype(jnp.float32), axis=-1)
        grad_norm = jnp.dot(tok_mat.T, returned, preferred_element_type=jnp.float32)
        inner = jnp.mean(grad_norm * x_float, axis=-1, keepdims=True)
        grad_in = grad_float + scale * grad_norm - x_float * (scale * scale * scale) * inner
        return grad_in.astype(jnp.bfloat16), grad_mix

    last = section_count - 1
    seed_float = cotangent.reshape(tokens, width).astype(jnp.float32)
    layer_in = inputs.reshape(tokens, width)
    outs = []
    saves = []
    grads_in = [None] * section_count
    mixes = [None] * section_count
    kepts = [None] * section_count
    for step in range(section_count):
        if step > 0:
            layer_in = hop(outs[-1], "section", step - 1, step)
        x_float = layer_in.astype(jnp.float32)
        scale = lax.rsqrt(jnp.mean(x_float * x_float, axis=-1, keepdims=True) + EPS)
        normed = (x_float * scale).astype(jnp.bfloat16)
        buffer = jnp.dot(tok_mat, normed, preferred_element_type=jnp.float32).astype(jnp.bfloat16)
        if step == 0:
            buffer = jnp.where(section_index == last, grad_buffer(seed_float), buffer)
        received = to_experts(all_to_all(buffer, devices, width))
        if step == 0:
            early_grad = received
        gate_pre, up_pre, hidden, results = expert_forward(received)
        if step == last:
            grad_back, grad_gate_pre, grad_up_pre = expert_backward(early_grad, gate_pre, up_pre)
            both = jnp.stack(
                [results.reshape(devices, -1, width), grad_back.reshape(devices, -1, width)], axis=1
            )
            back = lax.all_to_all(both, "expert", split_axis=0, concat_axis=0, tiled=True)
            returned = back[:, 0].reshape(-1, width)
            returned_grad = back[:, 1].reshape(-1, width)
            mixed, gathered = token_forward(x_float, returned)
            grads_in[step], mixes[step] = token_backward(
                seed_float, x_float, scale, gathered, returned_grad
            )
            kepts[step] = (received, early_grad, grad_gate_pre, grad_up_pre, hidden)
        else:
            returned = all_to_all(results.reshape(-1, width), devices, width)
            mixed, gathered = token_forward(x_float, returned)
        outs.append(mixed)
        saves.append((x_float, scale, received, gate_pre, up_pre, hidden, gathered))
    for step in reversed(range(last)):
        grad_out = hop(grads_in[step + 1], "section", step + 1, step)
        x_float, scale, received, gate_pre, up_pre, hidden, gathered = saves[step]
        grad_float = grad_out.astype(jnp.float32)
        grad_received = to_experts(all_to_all(grad_buffer(grad_float), devices, width))
        grad_back, grad_gate_pre, grad_up_pre = expert_backward(grad_received, gate_pre, up_pre)
        returned = all_to_all(grad_back.reshape(-1, width), devices, width)
        grads_in[step], mixes[step] = token_backward(grad_float, x_float, scale, gathered, returned)
        kepts[step] = (received, grad_received, grad_gate_pre, grad_up_pre, hidden)

    def pick(values):
        result = values[0]
        for step in range(1, section_count):
            result = jnp.where(section_index == step, values[step], result)
        return result

    def weight_grads(kept):
        received, grad_received, grad_gate_pre, grad_up_pre, hidden = kept
        grad_gate = jnp.einsum(
            "nemd,nemf->edf", received, grad_gate_pre, preferred_element_type=jnp.float32
        )
        grad_up = jnp.einsum("nemd,nemf->edf", received, grad_up_pre, preferred_element_type=jnp.float32)
        grad_down = jnp.einsum(
            "nemf,nemd->efd", hidden, grad_received, preferred_element_type=jnp.float32
        )
        return (
            grad_gate.astype(jnp.bfloat16),
            grad_up.astype(jnp.bfloat16),
            grad_down.astype(jnp.bfloat16),
        )

    branches = [lambda k=k: weight_grads(kepts[k]) for k in range(section_count)]
    grad_gate, grad_up, grad_down = lax.switch(section_index, branches)
    section_out = pick(outs).reshape(1, micro_count, tok_count, width)
    grad_input = pick(grads_in).reshape(1, micro_count, tok_count, width)
    grad_gates = pick(mixes).reshape(1, micro_count, tok_count, top_count)
    return (
        section_out,
        grad_input,
        grad_gates,
        grad_gate[None],
        grad_up[None],
        grad_down[None],
    )


def solution(mesh):
    in_specs = (
        P(None, "expert", None),
        P("section", None, "expert", None),
        P("section", None, "expert", None),
        P("section", "expert", None, None),
        P("section", "expert", None, None),
        P("section", "expert", None, None),
        P(None, "expert", None),
    )
    out_specs = (
        P("section", None, "expert", None),
        P("section", None, "expert", None),
        P("section", None, "expert", None),
        P("section", "expert", None, None),
        P("section", "expert", None, None),
        P("section", "expert", None, None),
    )
    return jax.shard_map(body, mesh=mesh, in_specs=in_specs, out_specs=out_specs, check_vma=False)
```

```python
import jax
import jax.numpy as jnp
from jax import lax
from jax.sharding import PartitionSpec as P

EPS = 1e-06


def hop(value, axis, source, target):
    return lax.ppermute(value, axis, [(source, target)])


def slot_matrices(ids, expert_count, most):
    micro_count, tok_count, top_count = ids.shape
    per_mb = tok_count * top_count
    flat = ids.reshape(micro_count, per_mb)
    order = jnp.arange(per_mb)
    earlier = order[:, None] > order[None, :]
    same = flat[:, :, None] == flat[:, None, :]
    position = jnp.sum(same & earlier[None], axis=2).astype(jnp.int32)
    micro = jnp.arange(micro_count, dtype=jnp.int32)[:, None]
    slot = flat * (micro_count * most) + micro * most + position
    slot = slot.reshape(-1)
    total_slots = expert_count * micro_count * most
    rows_mat = (jnp.arange(total_slots, dtype=jnp.int32)[:, None] == slot[None, :]).astype(jnp.bfloat16)
    tok_mat = rows_mat.reshape(total_slots, micro_count * tok_count, top_count).sum(axis=2)
    return rows_mat, tok_mat.astype(jnp.bfloat16)


def all_to_all(buffer, devices, width):
    shaped = buffer.reshape(devices, -1, width)
    out = lax.all_to_all(shaped, "expert", split_axis=0, concat_axis=0, tiled=True)
    return out.reshape(-1, width)


def body(inputs, route_ids, route_gates, w_gate, w_up, w_down, cotangent):
    section_count = lax.axis_size("section")
    section_index = lax.axis_index("section")
    devices = lax.axis_size("expert")
    micro_count, tok_count, width = inputs.shape
    top_count = route_ids.shape[3]
    exp_dev = w_gate.shape[1]
    hidden_width = w_gate.shape[3]
    expert_count = exp_dev * devices
    most = min(tok_count, 2 * tok_count * top_count // expert_count)
    slots_per = micro_count * most
    tokens = micro_count * tok_count
    gate_mat, up_mat, down_mat = (w_gate[0], w_up[0], w_down[0])
    ids = route_ids[0]
    gates = route_gates[0].reshape(tokens, top_count)
    rows_mat, tok_mat = slot_matrices(ids, expert_count, most)

    def to_experts(rows):
        return rows.reshape(devices, exp_dev, slots_per, -1)

    def expert_forward(received):
        gate_pre = jnp.einsum("nemd,edf->nemf", received, gate_mat, preferred_element_type=jnp.float32)
        up_pre = jnp.einsum("nemd,edf->nemf", received, up_mat, preferred_element_type=jnp.float32)
        hidden = (gate_pre * jax.nn.sigmoid(gate_pre) * up_pre).astype(jnp.bfloat16)
        results = jnp.einsum(
            "nemf,efd->nemd", hidden, down_mat, preferred_element_type=jnp.float32
        ).astype(jnp.bfloat16)
        return gate_pre, up_pre, hidden, results

    def hidden_grad(grad_received):
        return jnp.einsum("nemd,efd->nemf", grad_received, down_mat, preferred_element_type=jnp.float32)

    def expert_backward(grad_hidden, gate_pre, up_pre):
        sigma = jax.nn.sigmoid(gate_pre)
        active = gate_pre * sigma
        grad_gate_pre = (grad_hidden * up_pre * sigma * (1.0 + gate_pre * (1.0 - sigma))).astype(
            jnp.bfloat16
        )
        grad_up_pre = (grad_hidden * active).astype(jnp.bfloat16)
        grad_back = (
            jnp.einsum("nemf,edf->nemd", grad_gate_pre, gate_mat, preferred_element_type=jnp.float32)
            + jnp.einsum("nemf,edf->nemd", grad_up_pre, up_mat, preferred_element_type=jnp.float32)
        ).astype(jnp.bfloat16)
        return grad_back, grad_gate_pre, grad_up_pre

    def grad_buffer(grad_float):
        grad_rows = (gates[:, :, None] * grad_float[:, None, :]).astype(jnp.bfloat16).reshape(-1, width)
        return jnp.dot(rows_mat, grad_rows, preferred_element_type=jnp.float32).astype(jnp.bfloat16)

    def token_forward(x_float, returned):
        gathered = jnp.dot(rows_mat.T, returned, preferred_element_type=jnp.float32).astype(jnp.bfloat16)
        gathered = gathered.reshape(tokens, top_count, width)
        mixed = x_float + jnp.sum(gates[:, :, None] * gathered.astype(jnp.float32), axis=1)
        return mixed.astype(jnp.bfloat16), gathered

    def token_backward(grad_float, x_float, scale, gathered, returned):
        grad_mix = jnp.sum(grad_float[:, None, :] * gathered.astype(jnp.float32), axis=-1)
        grad_norm = jnp.dot(tok_mat.T, returned, preferred_element_type=jnp.float32)
        inner = jnp.mean(grad_norm * x_float, axis=-1, keepdims=True)
        grad_in = grad_float + scale * grad_norm - x_float * (scale * scale * scale) * inner
        return grad_in.astype(jnp.bfloat16), grad_mix

    last = section_count - 1
    seed_float = cotangent.reshape(tokens, width).astype(jnp.float32)
    layer_in = inputs.reshape(tokens, width)
    outs = []
    saves = []
    grads_in = [None] * section_count
    mixes = [None] * section_count
    kepts = [None] * section_count
    for step in range(section_count):
        if step > 0:
            layer_in = hop(outs[-1], "section", step - 1, step)
        x_float = layer_in.astype(jnp.float32)
        scale = lax.rsqrt(jnp.mean(x_float * x_float, axis=-1, keepdims=True) + EPS)
        normed = (x_float * scale).astype(jnp.bfloat16)
        if step == 0:
            buffer = lax.cond(
                section_index == last,
                lambda: grad_buffer(seed_float),
                lambda: jnp.dot(tok_mat, normed, preferred_element_type=jnp.float32).astype(
                    jnp.bfloat16
                ),
            )
        else:
            buffer = jnp.dot(tok_mat, normed, preferred_element_type=jnp.float32).astype(jnp.bfloat16)
        received = to_experts(all_to_all(buffer, devices, width))
        if step == 0:
            early_grad = received
            early_hidden = lax.cond(
                section_index == last,
                hidden_grad,
                lambda g: jnp.zeros(g.shape[:3] + (hidden_width,), jnp.float32),
                early_grad,
            )
        gate_pre, up_pre, hidden, results = expert_forward(received)
        if step == last:
            grad_back, grad_gate_pre, grad_up_pre = expert_backward(early_hidden, gate_pre, up_pre)
            both = jnp.stack(
                [results.reshape(devices, -1, width), grad_back.reshape(devices, -1, width)], axis=1
            )
            back = lax.all_to_all(both, "expert", split_axis=0, concat_axis=0, tiled=True)
            returned = back[:, 0].reshape(-1, width)
            returned_grad = back[:, 1].reshape(-1, width)
            mixed, gathered = token_forward(x_float, returned)
            grads_in[step], mixes[step] = token_backward(
                seed_float, x_float, scale, gathered, returned_grad
            )
            kepts[step] = (received, early_grad, grad_gate_pre, grad_up_pre, hidden)
        else:
            returned = all_to_all(results.reshape(-1, width), devices, width)
            mixed, gathered = token_forward(x_float, returned)
        outs.append(mixed)
        saves.append((x_float, scale, received, gate_pre, up_pre, hidden, gathered))
    for step in reversed(range(last)):
        grad_out = hop(grads_in[step + 1], "section", step + 1, step)
        x_float, scale, received, gate_pre, up_pre, hidden, gathered = saves[step]
        grad_float = grad_out.astype(jnp.float32)
        grad_received = to_experts(all_to_all(grad_buffer(grad_float), devices, width))
        grad_back, grad_gate_pre, grad_up_pre = expert_backward(
            hidden_grad(grad_received), gate_pre, up_pre
        )
        returned = all_to_all(grad_back.reshape(-1, width), devices, width)
        grads_in[step], mixes[step] = token_backward(grad_float, x_float, scale, gathered, returned)
        kepts[step] = (received, grad_received, grad_gate_pre, grad_up_pre, hidden)

    def pick(values):
        result = values[0]
        for step in range(1, section_count):
            result = jnp.where(section_index == step, values[step], result)
        return result

    def weight_grads(kept):
        received, grad_received, grad_gate_pre, grad_up_pre, hidden = kept
        grad_gate = jnp.einsum(
            "nemd,nemf->edf", received, grad_gate_pre, preferred_element_type=jnp.float32
        )
        grad_up = jnp.einsum("nemd,nemf->edf", received, grad_up_pre, preferred_element_type=jnp.float32)
        grad_down = jnp.einsum(
            "nemf,nemd->efd", hidden, grad_received, preferred_element_type=jnp.float32
        )
        return (
            grad_gate.astype(jnp.bfloat16),
            grad_up.astype(jnp.bfloat16),
            grad_down.astype(jnp.bfloat16),
        )

    grad_gate, grad_up, grad_down = weight_grads(
        tuple(pick([kept[i] for kept in kepts]) for i in range(len(kepts[0])))
    )
    section_out = pick(outs).reshape(1, micro_count, tok_count, width)
    grad_input = pick(grads_in).reshape(1, micro_count, tok_count, width)
    grad_gates = pick(mixes).reshape(1, micro_count, tok_count, top_count)
    return (
        section_out,
        grad_input,
        grad_gates,
        grad_gate[None],
        grad_up[None],
        grad_down[None],
    )


def solution(mesh):
    in_specs = (
        P(None, "expert", None),
        P("section", None, "expert", None),
        P("section", None, "expert", None),
        P("section", "expert", None, None),
        P("section", "expert", None, None),
        P("section", "expert", None, None),
        P(None, "expert", None),
    )
    out_specs = (
        P("section", None, "expert", None),
        P("section", None, "expert", None),
        P("section", None, "expert", None),
        P("section", "expert", None, None),
        P("section", "expert", None, None),
        P("section", "expert", None, None),
    )
    return jax.shard_map(body, mesh=mesh, in_specs=in_specs, out_specs=out_specs, check_vma=False)
```

```python
import jax
import jax.numpy as jnp
from jax import lax
from jax.sharding import PartitionSpec as P

EPS = 1e-06


def hop(value, axis, source, target):
    return lax.ppermute(value, axis, [(source, target)])


def slot_matrices(ids, expert_count, most):
    micro_count, tok_count, top_count = ids.shape
    per_mb = tok_count * top_count
    flat = ids.reshape(micro_count, per_mb)
    order = jnp.arange(per_mb)
    earlier = order[:, None] > order[None, :]
    same = flat[:, :, None] == flat[:, None, :]
    position = jnp.sum(same & earlier[None], axis=2).astype(jnp.int32)
    micro = jnp.arange(micro_count, dtype=jnp.int32)[:, None]
    slot = flat * (micro_count * most) + micro * most + position
    slot = slot.reshape(-1)
    total_slots = expert_count * micro_count * most
    rows_mat = (jnp.arange(total_slots, dtype=jnp.int32)[:, None] == slot[None, :]).astype(jnp.bfloat16)
    tok_mat = rows_mat.reshape(total_slots, micro_count * tok_count, top_count).sum(axis=2)
    return rows_mat, tok_mat.astype(jnp.bfloat16)


def all_to_all(buffer, devices, width):
    shaped = buffer.reshape(devices, -1, width)
    out = lax.all_to_all(shaped, "expert", split_axis=0, concat_axis=0, tiled=True)
    return out.reshape(-1, width)


def choose(index, values):
    result = values[0]
    for position in range(1, len(values)):
        result = jax.tree.map(
            lambda new, old, p=position: jnp.where(index == p, new, old), values[position], result
        )
    return result


def body(inputs, route_ids, route_gates, w_gate, w_up, w_down, cotangent):
    section_count = lax.axis_size("section")
    section_index = lax.axis_index("section")
    devices = lax.axis_size("expert")
    micro_count, tok_count, width = inputs.shape
    top_count = route_ids.shape[3]
    exp_dev = w_gate.shape[1]
    expert_count = exp_dev * devices
    most = min(tok_count, 2 * tok_count * top_count // expert_count)
    gate_mat, up_mat, down_mat = (w_gate[0], w_up[0], w_down[0])
    ids = route_ids[0]
    gates_all = route_gates[0]
    mats = [slot_matrices(ids[m][None], expert_count, most) for m in range(micro_count)]
    last = section_count - 1
    ticks = 2 * last + micro_count
    is_last = section_index == last

    def role(t, s):
        if s == last:
            m = t - last
            return ("FB", m) if 0 <= m < micro_count else None
        if 0 <= t - s < micro_count:
            return ("F", t - s)
        m = t - 2 * last + s
        return ("B", m) if 0 <= m < micro_count else None

    for t in range(ticks):
        for s in range(last):
            assert not (0 <= t - s < micro_count and 0 <= t - 2 * last + s < micro_count)

    def to_experts(rows):
        return rows.reshape(devices, exp_dev, most, -1)

    def expert_forward(received):
        gate_pre = jnp.einsum("nemd,edf->nemf", received, gate_mat, preferred_element_type=jnp.float32)
        up_pre = jnp.einsum("nemd,edf->nemf", received, up_mat, preferred_element_type=jnp.float32)
        hidden = (gate_pre * jax.nn.sigmoid(gate_pre) * up_pre).astype(jnp.bfloat16)
        results = jnp.einsum(
            "nemf,efd->nemd", hidden, down_mat, preferred_element_type=jnp.float32
        ).astype(jnp.bfloat16)
        return gate_pre, up_pre, hidden, results

    def expert_backward(grad_received, gate_pre, up_pre):
        sigma = jax.nn.sigmoid(gate_pre)
        active = gate_pre * sigma
        grad_hidden = jnp.einsum(
            "nemd,efd->nemf", grad_received, down_mat, preferred_element_type=jnp.float32
        )
        grad_gate_pre = (grad_hidden * up_pre * sigma * (1.0 + gate_pre * (1.0 - sigma))).astype(
            jnp.bfloat16
        )
        grad_up_pre = (grad_hidden * active).astype(jnp.bfloat16)
        grad_back = (
            jnp.einsum("nemf,edf->nemd", grad_gate_pre, gate_mat, preferred_element_type=jnp.float32)
            + jnp.einsum("nemf,edf->nemd", grad_up_pre, up_mat, preferred_element_type=jnp.float32)
        ).astype(jnp.bfloat16)
        return grad_back, grad_gate_pre, grad_up_pre

    def grad_buffer(grad_float, gates, rows_mat):
        grad_rows = (gates[:, :, None] * grad_float[:, None, :]).astype(jnp.bfloat16).reshape(-1, width)
        return jnp.dot(rows_mat, grad_rows, preferred_element_type=jnp.float32).astype(jnp.bfloat16)

    fsave = {}
    early = {}
    kept = {}
    fwd_out = {}
    bwd_out = {}
    incoming = None
    for t in range(ticks):
        roles = [role(t, s) for s in range(section_count)]
        has_f = any(r is not None and r[0] in ("F", "FB") for r in roles)
        has_b = any(r is not None and r[0] in ("B", "FB") for r in roles)
        micro = jnp.int32(0)
        for s, r in enumerate(roles):
            if r is not None:
                micro = jnp.where(section_index == s, r[1], micro)
        rows_mat = choose(micro, [mat[0] for mat in mats])
        tok_mat = choose(micro, [mat[1] for mat in mats])
        gates = choose(micro, [gates_all[m] for m in range(micro_count)])
        b_role = jnp.bool_(False)
        for s, r in enumerate(roles):
            if r is not None and r[0] == "B":
                b_role = b_role | (section_index == s)
        saved = None
        sources = [(s, s + r[1]) for s, r in enumerate(roles) if r is not None and r[0] == "B"]
        if sources:
            saved = fsave[sources[0][1]]
            for s, tick in sources[1:]:
                saved = jax.tree.map(
                    lambda new, old, s=s: jnp.where(section_index == s, new, old), fsave[tick], saved
                )
        if has_f:
            first_in = choose(micro, [inputs[m] for m in range(micro_count)])
            x_in = first_in if incoming is None else jnp.where(section_index == 0, first_in, incoming)
            x_float = x_in.astype(jnp.float32)
            scale = lax.rsqrt(jnp.mean(x_float * x_float, axis=-1, keepdims=True) + EPS)
            normed = (x_float * scale).astype(jnp.bfloat16)
            buffer = jnp.dot(tok_mat, normed, preferred_element_type=jnp.float32).astype(jnp.bfloat16)
            if roles[last] is None and t < micro_count:
                pre = grad_buffer(cotangent[t].astype(jnp.float32), gates_all[t], mats[t][0])
                buffer = jnp.where(is_last, pre, buffer)
        if has_b:
            seed = choose(micro, [cotangent[m] for m in range(micro_count)])
            grad_in_now = seed if incoming is None else jnp.where(is_last, seed, incoming)
            grad_float = grad_in_now.astype(jnp.float32)
            bbuf = grad_buffer(grad_float, gates, rows_mat)
            buffer = jnp.where(b_role, bbuf, buffer) if has_f else bbuf
        received = to_experts(all_to_all(buffer, devices, width))
        if roles[last] is None and t < micro_count:
            early[t] = received
        if has_f:
            gate_pre, up_pre, hidden, results = expert_forward(received)
        if has_b:
            if roles[last] is not None:
                g_src = early[roles[last][1]]
                if saved is None:
                    g_rows, g_gate, g_up = g_src, gate_pre, up_pre
                else:
                    g_rows = jnp.where(is_last, g_src, received)
                    g_gate = jnp.where(is_last, gate_pre, saved[3])
                    g_up = jnp.where(is_last, up_pre, saved[4])
            else:
                g_rows, g_gate, g_up = received, saved[3], saved[4]
            grad_back, grad_gate_pre, grad_up_pre = expert_backward(g_rows, g_gate, g_up)
            kept[t] = (received, grad_gate_pre, grad_up_pre)
        if has_f and has_b:
            both = jnp.stack(
                [results.reshape(devices, -1, width), grad_back.reshape(devices, -1, width)], axis=1
            )
            back = lax.all_to_all(both, "expert", split_axis=0, concat_axis=0, tiled=True)
            returned_f = back[:, 0].reshape(-1, width)
            returned_b = back[:, 1].reshape(-1, width)
        elif has_f:
            returned_f = all_to_all(results.reshape(-1, width), devices, width)
        else:
            returned_b = all_to_all(grad_back.reshape(-1, width), devices, width)
        if has_f:
            gathered = jnp.dot(rows_mat.T, returned_f, preferred_element_type=jnp.float32).astype(
                jnp.bfloat16
            )
            gathered = gathered.reshape(tok_count, top_count, width)
            mixed = x_float + jnp.sum(gates[:, :, None] * gathered.astype(jnp.float32), axis=1)
            mixed = mixed.astype(jnp.bfloat16)
            fsave[t] = (x_float, scale, received, gate_pre, up_pre, hidden, gathered)
            fwd_out[t] = mixed
        if has_b:
            if roles[last] is not None:
                if saved is None:
                    bx, bscale, bgathered = x_float, scale, gathered
                else:
                    bx = jnp.where(is_last, x_float, saved[0])
                    bscale = jnp.where(is_last, scale, saved[1])
                    bgathered = jnp.where(is_last, gathered, saved[6])
            else:
                bx, bscale, bgathered = saved[0], saved[1], saved[6]
            grad_mix = jnp.sum(grad_float[:, None, :] * bgathered.astype(jnp.float32), axis=-1)
            grad_norm = jnp.dot(tok_mat.T, returned_b, preferred_element_type=jnp.float32)
            inner = jnp.mean(grad_norm * bx, axis=-1, keepdims=True)
            grad_in = grad_float + bscale * grad_norm - bx * (bscale * bscale * bscale) * inner
            grad_in = grad_in.astype(jnp.bfloat16)
            bwd_out[t] = (grad_in, grad_mix)
        if t < ticks - 1:
            pairs = []
            for s, r in enumerate(roles):
                if r is None:
                    continue
                if r[0] == "F":
                    pairs.append((s, s + 1))
                elif s > 0:
                    pairs.append((s, s - 1))
            if has_f and has_b:
                f_role = jnp.bool_(False)
                for s, r in enumerate(roles):
                    if r is not None and r[0] == "F":
                        f_role = f_role | (section_index == s)
                send = jnp.where(f_role, mixed, grad_in)
            elif has_f:
                send = mixed
            else:
                send = grad_in
            incoming = lax.ppermute(send, "section", pairs)

    def b_tick(s, m):
        return last + m if s == last else 2 * last - s + m

    section_out = jnp.stack(
        [choose(section_index, [fwd_out[s + m] for s in range(section_count)]) for m in range(micro_count)]
    )
    grad_input = jnp.stack(
        [
            choose(section_index, [bwd_out[b_tick(s, m)][0] for s in range(section_count)])
            for m in range(micro_count)
        ]
    )
    grad_gates = jnp.stack(
        [
            choose(section_index, [bwd_out[b_tick(s, m)][1] for s in range(section_count)])
            for m in range(micro_count)
        ]
    )

    def weight_grads(s):
        rows = []
        grows = []
        ggps = []
        gups = []
        hids = []
        for m in range(micro_count):
            tick = b_tick(s, m)
            received, grad_gate_pre, grad_up_pre = kept[tick]
            fwd = fsave[s + m]
            rows.append(fwd[2])
            hids.append(fwd[5])
            grows.append(early[m] if s == last else received)
            ggps.append(grad_gate_pre)
            gups.append(grad_up_pre)
        cat = lambda parts: jnp.concatenate(parts, axis=2)
        rows, grows, ggps, gups, hids = map(cat, (rows, grows, ggps, gups, hids))
        grad_gate = jnp.einsum("nemd,nemf->edf", rows, ggps, preferred_element_type=jnp.float32)
        grad_up = jnp.einsum("nemd,nemf->edf", rows, gups, preferred_element_type=jnp.float32)
        grad_down = jnp.einsum("nemf,nemd->efd", hids, grows, preferred_element_type=jnp.float32)
        return (
            grad_gate.astype(jnp.bfloat16),
            grad_up.astype(jnp.bfloat16),
            grad_down.astype(jnp.bfloat16),
        )

    branches = [lambda s=s: weight_grads(s) for s in range(section_count)]
    grad_gate, grad_up, grad_down = lax.switch(section_index, branches)
    return (
        section_out[None],
        grad_input[None],
        grad_gates[None],
        grad_gate[None],
        grad_up[None],
        grad_down[None],
    )


def solution(mesh):
    in_specs = (
        P(None, "expert", None),
        P("section", None, "expert", None),
        P("section", None, "expert", None),
        P("section", "expert", None, None),
        P("section", "expert", None, None),
        P("section", "expert", None, None),
        P(None, "expert", None),
    )
    out_specs = (
        P("section", None, "expert", None),
        P("section", None, "expert", None),
        P("section", None, "expert", None),
        P("section", "expert", None, None),
        P("section", "expert", None, None),
        P("section", "expert", None, None),
    )
    return jax.shard_map(body, mesh=mesh, in_specs=in_specs, out_specs=out_specs, check_vma=False)
```

```python
import jax
import jax.numpy as jnp
from jax import lax
from jax.sharding import PartitionSpec as P

EPS = 1e-06


def hop(value, axis, source, target):
    return lax.ppermute(value, axis, [(source, target)])


def slot_matrices(ids, expert_count, most):
    micro_count, tok_count, top_count = ids.shape
    per_mb = tok_count * top_count
    flat = ids.reshape(micro_count, per_mb)
    order = jnp.arange(per_mb)
    earlier = order[:, None] > order[None, :]
    same = flat[:, :, None] == flat[:, None, :]
    position = jnp.sum(same & earlier[None], axis=2).astype(jnp.int32)
    micro = jnp.arange(micro_count, dtype=jnp.int32)[:, None]
    slot = flat * (micro_count * most) + micro * most + position
    slot = slot.reshape(-1)
    total_slots = expert_count * micro_count * most
    rows_mat = (jnp.arange(total_slots, dtype=jnp.int32)[:, None] == slot[None, :]).astype(jnp.bfloat16)
    tok_mat = rows_mat.reshape(total_slots, micro_count * tok_count, top_count).sum(axis=2)
    return rows_mat, tok_mat.astype(jnp.bfloat16)


def all_to_all(buffer, devices, width):
    shaped = buffer.reshape(devices, -1, width)
    out = lax.all_to_all(shaped, "expert", split_axis=0, concat_axis=0, tiled=True)
    return out.reshape(-1, width)


def body(inputs, route_ids, route_gates, w_gate, w_up, w_down, cotangent):
    section_count = lax.axis_size("section")
    section_index = lax.axis_index("section")
    devices = lax.axis_size("expert")
    micro_count, tok_count, width = inputs.shape
    top_count = route_ids.shape[3]
    exp_dev = w_gate.shape[1]
    hidden_width = w_gate.shape[3]
    expert_count = exp_dev * devices
    most = min(tok_count, 2 * tok_count * top_count // expert_count)
    slots_per = micro_count * most
    tokens = micro_count * tok_count
    gate_mat, up_mat, down_mat = (w_gate[0], w_up[0], w_down[0])
    ids = route_ids[0]
    gates = route_gates[0].reshape(tokens, top_count)
    rows_mat, tok_mat = slot_matrices(ids, expert_count, most)

    def to_experts(rows):
        return rows.reshape(devices, exp_dev, slots_per, -1)

    def expert_forward(received):
        gate_pre = jnp.einsum("nemd,edf->nemf", received, gate_mat, preferred_element_type=jnp.float32)
        up_pre = jnp.einsum("nemd,edf->nemf", received, up_mat, preferred_element_type=jnp.float32)
        hidden = (gate_pre * jax.nn.sigmoid(gate_pre) * up_pre).astype(jnp.bfloat16)
        results = jnp.einsum(
            "nemf,efd->nemd", hidden, down_mat, preferred_element_type=jnp.float32
        ).astype(jnp.bfloat16)
        return gate_pre, up_pre, hidden, results

    def expert_backward(grad_received, gate_pre, up_pre):
        sigma = jax.nn.sigmoid(gate_pre)
        active = gate_pre * sigma
        grad_hidden = jnp.einsum(
            "nemd,efd->nemf", grad_received, down_mat, preferred_element_type=jnp.float32
        )
        grad_gate_pre = (grad_hidden * up_pre * sigma * (1.0 + gate_pre * (1.0 - sigma))).astype(
            jnp.bfloat16
        )
        grad_up_pre = (grad_hidden * active).astype(jnp.bfloat16)
        grad_back = (
            jnp.einsum("nemf,edf->nemd", grad_gate_pre, gate_mat, preferred_element_type=jnp.float32)
            + jnp.einsum("nemf,edf->nemd", grad_up_pre, up_mat, preferred_element_type=jnp.float32)
        ).astype(jnp.bfloat16)
        return grad_back, grad_gate_pre, grad_up_pre

    def grad_buffer(grad_float):
        grad_rows = (gates[:, :, None] * grad_float[:, None, :]).astype(jnp.bfloat16).reshape(-1, width)
        return jnp.dot(rows_mat, grad_rows, preferred_element_type=jnp.float32).astype(jnp.bfloat16)

    def token_forward(x_float, returned):
        gathered = jnp.dot(rows_mat.T, returned, preferred_element_type=jnp.float32).astype(jnp.bfloat16)
        gathered = gathered.reshape(tokens, top_count, width)
        mixed = x_float + jnp.sum(gates[:, :, None] * gathered.astype(jnp.float32), axis=1)
        return mixed.astype(jnp.bfloat16), gathered

    def token_backward(grad_float, x_float, scale, gathered, returned):
        grad_mix = jnp.sum(grad_float[:, None, :] * gathered.astype(jnp.float32), axis=-1)
        grad_norm = jnp.dot(tok_mat.T, returned, preferred_element_type=jnp.float32)
        inner = jnp.mean(grad_norm * x_float, axis=-1, keepdims=True)
        grad_in = grad_float + scale * grad_norm - x_float * (scale * scale * scale) * inner
        return grad_in.astype(jnp.bfloat16), grad_mix

    last = section_count - 1
    early_step = min(1, last - 1)
    seed_float = cotangent.reshape(tokens, width).astype(jnp.float32)
    layer_in = inputs.reshape(tokens, width)
    outs = []
    saves = []
    grads_in = [None] * section_count
    mixes = [None] * section_count
    kepts = [None] * section_count
    for step in range(section_count):
        if step > 0:
            layer_in = hop(outs[-1], "section", step - 1, step)
        x_float = layer_in.astype(jnp.float32)
        scale = lax.rsqrt(jnp.mean(x_float * x_float, axis=-1, keepdims=True) + EPS)
        normed = (x_float * scale).astype(jnp.bfloat16)
        buffer = jnp.dot(tok_mat, normed, preferred_element_type=jnp.float32).astype(jnp.bfloat16)
        if step == early_step:
            buffer = jnp.where(section_index == last, grad_buffer(seed_float), buffer)
        received = to_experts(all_to_all(buffer, devices, width))
        if step == early_step:
            early_grad = received
        gate_pre, up_pre, hidden, results = expert_forward(received)
        if step == last:
            grad_back, grad_gate_pre, grad_up_pre = expert_backward(early_grad, gate_pre, up_pre)
            both = jnp.stack(
                [results.reshape(devices, -1, width), grad_back.reshape(devices, -1, width)], axis=1
            )
            back = lax.all_to_all(both, "expert", split_axis=0, concat_axis=0, tiled=True)
            returned = back[:, 0].reshape(-1, width)
            returned_grad = back[:, 1].reshape(-1, width)
            mixed, gathered = token_forward(x_float, returned)
            grads_in[step], mixes[step] = token_backward(
                seed_float, x_float, scale, gathered, returned_grad
            )
            kepts[step] = (received, early_grad, grad_gate_pre, grad_up_pre, hidden)
        else:
            returned = all_to_all(results.reshape(-1, width), devices, width)
            mixed, gathered = token_forward(x_float, returned)
        outs.append(mixed)
        saves.append((x_float, scale, received, gate_pre, up_pre, hidden, gathered))
    for step in reversed(range(last)):
        grad_out = hop(grads_in[step + 1], "section", step + 1, step)
        x_float, scale, received, gate_pre, up_pre, hidden, gathered = saves[step]
        grad_float = grad_out.astype(jnp.float32)
        grad_received = to_experts(all_to_all(grad_buffer(grad_float), devices, width))
        grad_back, grad_gate_pre, grad_up_pre = expert_backward(grad_received, gate_pre, up_pre)
        returned = all_to_all(grad_back.reshape(-1, width), devices, width)
        grads_in[step], mixes[step] = token_backward(grad_float, x_float, scale, gathered, returned)
        kepts[step] = (received, grad_received, grad_gate_pre, grad_up_pre, hidden)

    def pick(values):
        result = values[0]
        for step in range(1, section_count):
            result = jnp.where(section_index == step, values[step], result)
        return result

    def weight_grads(kept):
        received, grad_received, grad_gate_pre, grad_up_pre, hidden = kept
        grad_gate = jnp.einsum(
            "nemd,nemf->edf", received, grad_gate_pre, preferred_element_type=jnp.float32
        )
        grad_up = jnp.einsum("nemd,nemf->edf", received, grad_up_pre, preferred_element_type=jnp.float32)
        grad_down = jnp.einsum(
            "nemf,nemd->efd", hidden, grad_received, preferred_element_type=jnp.float32
        )
        return (
            grad_gate.astype(jnp.bfloat16),
            grad_up.astype(jnp.bfloat16),
            grad_down.astype(jnp.bfloat16),
        )

    branches = [lambda k=k: weight_grads(kepts[k]) for k in range(section_count)]
    grad_gate, grad_up, grad_down = lax.switch(section_index, branches)
    section_out = pick(outs).reshape(1, micro_count, tok_count, width)
    grad_input = pick(grads_in).reshape(1, micro_count, tok_count, width)
    grad_gates = pick(mixes).reshape(1, micro_count, tok_count, top_count)
    return (
        section_out,
        grad_input,
        grad_gates,
        grad_gate[None],
        grad_up[None],
        grad_down[None],
    )


def solution(mesh):
    in_specs = (
        P(None, "expert", None),
        P("section", None, "expert", None),
        P("section", None, "expert", None),
        P("section", "expert", None, None),
        P("section", "expert", None, None),
        P("section", "expert", None, None),
        P(None, "expert", None),
    )
    out_specs = (
        P("section", None, "expert", None),
        P("section", None, "expert", None),
        P("section", None, "expert", None),
        P("section", "expert", None, None),
        P("section", "expert", None, None),
        P("section", "expert", None, None),
    )
    return jax.shard_map(body, mesh=mesh, in_specs=in_specs, out_specs=out_specs, check_vma=False)
```

```python
import jax
import jax.numpy as jnp
from jax import lax
from jax.sharding import PartitionSpec as P

EPS = 1e-06


def hop(value, axis, source, target):
    return lax.ppermute(value, axis, [(source, target)])


def slot_matrices(ids, expert_count, most):
    micro_count, tok_count, top_count = ids.shape
    per_mb = tok_count * top_count
    flat = ids.reshape(micro_count, per_mb)
    order = jnp.arange(per_mb)
    earlier = order[:, None] > order[None, :]
    same = flat[:, :, None] == flat[:, None, :]
    position = jnp.sum(same & earlier[None], axis=2).astype(jnp.int32)
    micro = jnp.arange(micro_count, dtype=jnp.int32)[:, None]
    slot = flat * (micro_count * most) + micro * most + position
    slot = slot.reshape(-1)
    total_slots = expert_count * micro_count * most
    rows_mat = (jnp.arange(total_slots, dtype=jnp.int32)[:, None] == slot[None, :]).astype(jnp.bfloat16)
    tok_mat = rows_mat.reshape(total_slots, micro_count * tok_count, top_count).sum(axis=2)
    return rows_mat, tok_mat.astype(jnp.bfloat16)


def all_to_all(buffer, devices, width):
    shaped = buffer.reshape(devices, -1, width)
    out = lax.all_to_all(shaped, "expert", split_axis=0, concat_axis=0, tiled=True)
    return out.reshape(-1, width)


def body(inputs, route_ids, route_gates, w_gate, w_up, w_down, cotangent):
    section_count = lax.axis_size("section")
    section_index = lax.axis_index("section")
    devices = lax.axis_size("expert")
    micro_count, tok_count, width = inputs.shape
    top_count = route_ids.shape[3]
    exp_dev = w_gate.shape[1]
    hidden_width = w_gate.shape[3]
    expert_count = exp_dev * devices
    most = min(tok_count, 2 * tok_count * top_count // expert_count)
    slots_per = micro_count * most
    tokens = micro_count * tok_count
    gate_mat, up_mat, down_mat = (w_gate[0], w_up[0], w_down[0])
    ids = route_ids[0]
    gates = route_gates[0].reshape(tokens, top_count)
    rows_mat, tok_mat = slot_matrices(ids, expert_count, most)

    def to_experts(rows):
        return rows.reshape(devices, exp_dev, slots_per, -1)

    def expert_forward(received):
        gate_pre = jnp.einsum("nemd,edf->nemf", received, gate_mat, preferred_element_type=jnp.float32)
        up_pre = jnp.einsum("nemd,edf->nemf", received, up_mat, preferred_element_type=jnp.float32)
        hidden = (gate_pre * jax.nn.sigmoid(gate_pre) * up_pre).astype(jnp.bfloat16)
        results = jnp.einsum(
            "nemf,efd->nemd", hidden, down_mat, preferred_element_type=jnp.float32
        ).astype(jnp.bfloat16)
        return gate_pre, up_pre, hidden, results

    def expert_backward(grad_received, gate_pre, up_pre):
        sigma = jax.nn.sigmoid(gate_pre)
        active = gate_pre * sigma
        grad_hidden = jnp.einsum(
            "nemd,efd->nemf", grad_received, down_mat, preferred_element_type=jnp.float32
        )
        grad_gate_pre = (grad_hidden * up_pre * sigma * (1.0 + gate_pre * (1.0 - sigma))).astype(
            jnp.bfloat16
        )
        grad_up_pre = (grad_hidden * active).astype(jnp.bfloat16)
        grad_back = (
            jnp.einsum("nemf,edf->nemd", grad_gate_pre, gate_mat, preferred_element_type=jnp.float32)
            + jnp.einsum("nemf,edf->nemd", grad_up_pre, up_mat, preferred_element_type=jnp.float32)
        ).astype(jnp.bfloat16)
        return grad_back, grad_gate_pre, grad_up_pre

    def grad_buffer(grad_float):
        grad_rows = (gates[:, :, None] * grad_float[:, None, :]).astype(jnp.bfloat16).reshape(-1, width)
        return jnp.dot(rows_mat, grad_rows, preferred_element_type=jnp.float32).astype(jnp.bfloat16)

    def token_forward(x_float, returned):
        gathered = jnp.dot(rows_mat.T, returned, preferred_element_type=jnp.float32).astype(jnp.bfloat16)
        gathered = gathered.reshape(tokens, top_count, width)
        mixed = x_float + jnp.sum(gates[:, :, None] * gathered.astype(jnp.float32), axis=1)
        return mixed.astype(jnp.bfloat16), gathered

    def token_backward(grad_float, x_float, scale, gathered, returned):
        grad_mix = jnp.sum(grad_float[:, None, :] * gathered.astype(jnp.float32), axis=-1)
        grad_norm = jnp.dot(tok_mat.T, returned, preferred_element_type=jnp.float32)
        inner = jnp.mean(grad_norm * x_float, axis=-1, keepdims=True)
        grad_in = grad_float + scale * grad_norm - x_float * (scale * scale * scale) * inner
        return grad_in.astype(jnp.bfloat16), grad_mix

    last = section_count - 1
    early_step = min(1, last - 1)
    seed_float = cotangent.reshape(tokens, width).astype(jnp.float32)
    layer_in = inputs.reshape(tokens, width)
    outs = []
    saves = []
    grads_in = [None] * section_count
    mixes = [None] * section_count
    kepts = [None] * section_count
    for step in range(section_count):
        if step > 0:
            layer_in = hop(outs[-1], "section", step - 1, step)
        x_float = layer_in.astype(jnp.float32)
        scale = lax.rsqrt(jnp.mean(x_float * x_float, axis=-1, keepdims=True) + EPS)
        normed = (x_float * scale).astype(jnp.bfloat16)
        buffer = jnp.dot(tok_mat, normed, preferred_element_type=jnp.float32).astype(jnp.bfloat16)
        if step == early_step:
            buffer = jnp.where(section_index == last, grad_buffer(seed_float), buffer)
        received = to_experts(all_to_all(buffer, devices, width))
        if step == early_step:
            early_grad = received
        gate_pre, up_pre, hidden, results = expert_forward(received)
        if step == last:
            grad_back, grad_gate_pre, grad_up_pre = expert_backward(early_grad, gate_pre, up_pre)
            both = jnp.stack(
                [results.reshape(devices, -1, width), grad_back.reshape(devices, -1, width)], axis=1
            )
            back = lax.all_to_all(both, "expert", split_axis=0, concat_axis=0, tiled=True)
            returned = back[:, 0].reshape(-1, width)
            returned_grad = back[:, 1].reshape(-1, width)
            mixed, gathered = token_forward(x_float, returned)
            grads_in[step], mixes[step] = token_backward(
                seed_float, x_float, scale, gathered, returned_grad
            )
            kepts[step] = (received, early_grad, grad_gate_pre, grad_up_pre, hidden)
        else:
            returned = all_to_all(results.reshape(-1, width), devices, width)
            mixed, gathered = token_forward(x_float, returned)
        outs.append(mixed)
        saves.append((x_float, scale, received, gate_pre, up_pre, hidden, gathered))
    for step in reversed(range(last)):
        grad_out = hop(grads_in[step + 1], "section", step + 1, step)
        x_float, scale, received, gate_pre, up_pre, hidden, gathered = saves[step]
        grad_float = grad_out.astype(jnp.float32)
        grad_received = to_experts(all_to_all(grad_buffer(grad_float), devices, width))
        grad_back, grad_gate_pre, grad_up_pre = expert_backward(grad_received, gate_pre, up_pre)
        returned = all_to_all(grad_back.reshape(-1, width), devices, width)
        grads_in[step], mixes[step] = token_backward(grad_float, x_float, scale, gathered, returned)
        kepts[step] = (received, grad_received, grad_gate_pre, grad_up_pre, hidden)

    def pick(values):
        result = values[0]
        for step in range(1, section_count):
            result = jnp.where(section_index == step, values[step], result)
        return result

    def weight_grads(kept):
        received, grad_received, grad_gate_pre, grad_up_pre, hidden = kept
        grad_gate = jnp.einsum(
            "nemd,nemf->edf", received, grad_gate_pre, preferred_element_type=jnp.float32
        )
        grad_up = jnp.einsum("nemd,nemf->edf", received, grad_up_pre, preferred_element_type=jnp.float32)
        grad_down = jnp.einsum(
            "nemf,nemd->efd", hidden, grad_received, preferred_element_type=jnp.float32
        )
        return (
            grad_gate.astype(jnp.bfloat16),
            grad_up.astype(jnp.bfloat16),
            grad_down.astype(jnp.bfloat16),
        )

    branches = [lambda k=k: kepts[k] for k in range(section_count)]
    grad_gate, grad_up, grad_down = weight_grads(lax.switch(section_index, branches))
    section_out = pick(outs).reshape(1, micro_count, tok_count, width)
    grad_input = pick(grads_in).reshape(1, micro_count, tok_count, width)
    grad_gates = pick(mixes).reshape(1, micro_count, tok_count, top_count)
    return (
        section_out,
        grad_input,
        grad_gates,
        grad_gate[None],
        grad_up[None],
        grad_down[None],
    )


def solution(mesh):
    in_specs = (
        P(None, "expert", None),
        P("section", None, "expert", None),
        P("section", None, "expert", None),
        P("section", "expert", None, None),
        P("section", "expert", None, None),
        P("section", "expert", None, None),
        P(None, "expert", None),
    )
    out_specs = (
        P("section", None, "expert", None),
        P("section", None, "expert", None),
        P("section", None, "expert", None),
        P("section", "expert", None, None),
        P("section", "expert", None, None),
        P("section", "expert", None, None),
    )
    return jax.shard_map(body, mesh=mesh, in_specs=in_specs, out_specs=out_specs, check_vma=False)
```

```python
import jax
import jax.numpy as jnp
from jax import lax
from jax.sharding import PartitionSpec as P

EPS = 1e-06


def hop(value, axis, source, target):
    return lax.ppermute(value, axis, [(source, target)])


def slot_matrices(ids, expert_count, most):
    micro_count, tok_count, top_count = ids.shape
    per_mb = tok_count * top_count
    flat = ids.reshape(micro_count, per_mb)
    order = jnp.arange(per_mb)
    earlier = order[:, None] > order[None, :]
    same = flat[:, :, None] == flat[:, None, :]
    position = jnp.sum(same & earlier[None], axis=2).astype(jnp.int32)
    micro = jnp.arange(micro_count, dtype=jnp.int32)[:, None]
    slot = flat * (micro_count * most) + micro * most + position
    slot = slot.reshape(-1)
    total_slots = expert_count * micro_count * most
    rows_mat = (jnp.arange(total_slots, dtype=jnp.int32)[:, None] == slot[None, :]).astype(jnp.bfloat16)
    tok_mat = rows_mat.reshape(total_slots, micro_count * tok_count, top_count).sum(axis=2)
    return rows_mat, tok_mat.astype(jnp.bfloat16)


def all_to_all(buffer, devices, width):
    shaped = buffer.reshape(devices, -1, width)
    out = lax.all_to_all(shaped, "expert", split_axis=0, concat_axis=0, tiled=True)
    return out.reshape(-1, width)


def body(inputs, route_ids, route_gates, w_gate, w_up, w_down, cotangent):
    section_count = lax.axis_size("section")
    section_index = lax.axis_index("section")
    devices = lax.axis_size("expert")
    micro_count, tok_count, width = inputs.shape
    top_count = route_ids.shape[3]
    exp_dev = w_gate.shape[1]
    hidden_width = w_gate.shape[3]
    expert_count = exp_dev * devices
    most = min(tok_count, 2 * tok_count * top_count // expert_count)
    slots_per = micro_count * most
    tokens = micro_count * tok_count
    gate_mat, up_mat, down_mat = (w_gate[0], w_up[0], w_down[0])
    ids = route_ids[0]
    gates = route_gates[0].reshape(tokens, top_count)
    rows_mat, tok_mat = slot_matrices(ids, expert_count, most)
    mix_mat = (rows_mat.T.astype(jnp.float32) * gates.reshape(-1)[:, None]).reshape(
        tokens, top_count, -1
    ).sum(axis=1)

    def to_experts(rows):
        return rows.reshape(devices, exp_dev, slots_per, -1)

    def expert_forward(received):
        gate_pre = jnp.einsum("nemd,edf->nemf", received, gate_mat, preferred_element_type=jnp.float32)
        up_pre = jnp.einsum("nemd,edf->nemf", received, up_mat, preferred_element_type=jnp.float32)
        hidden = (gate_pre * jax.nn.sigmoid(gate_pre) * up_pre).astype(jnp.bfloat16)
        results = jnp.einsum(
            "nemf,efd->nemd", hidden, down_mat, preferred_element_type=jnp.float32
        ).astype(jnp.bfloat16)
        return gate_pre, up_pre, hidden, results

    def expert_backward(grad_received, gate_pre, up_pre):
        sigma = jax.nn.sigmoid(gate_pre)
        active = gate_pre * sigma
        grad_hidden = jnp.einsum(
            "nemd,efd->nemf", grad_received, down_mat, preferred_element_type=jnp.float32
        )
        grad_gate_pre = (grad_hidden * up_pre * sigma * (1.0 + gate_pre * (1.0 - sigma))).astype(
            jnp.bfloat16
        )
        grad_up_pre = (grad_hidden * active).astype(jnp.bfloat16)
        grad_back = (
            jnp.einsum("nemf,edf->nemd", grad_gate_pre, gate_mat, preferred_element_type=jnp.float32)
            + jnp.einsum("nemf,edf->nemd", grad_up_pre, up_mat, preferred_element_type=jnp.float32)
        ).astype(jnp.bfloat16)
        return grad_back, grad_gate_pre, grad_up_pre

    def grad_buffer(grad_float):
        grad_rows = (gates[:, :, None] * grad_float[:, None, :]).astype(jnp.bfloat16).reshape(-1, width)
        return jnp.dot(rows_mat, grad_rows, preferred_element_type=jnp.float32).astype(jnp.bfloat16)

    def token_forward(x_float, returned):
        gathered = jnp.dot(rows_mat.T, returned, preferred_element_type=jnp.float32).astype(jnp.bfloat16)
        gathered = gathered.reshape(tokens, top_count, width)
        mixed = x_float + jnp.dot(
            mix_mat,
            returned.astype(jnp.float32),
            precision=lax.Precision.HIGHEST,
            preferred_element_type=jnp.float32,
        )
        return mixed.astype(jnp.bfloat16), gathered

    def token_backward(grad_float, x_float, scale, gathered, returned):
        grad_mix = jnp.sum(grad_float[:, None, :] * gathered.astype(jnp.float32), axis=-1)
        grad_norm = jnp.dot(tok_mat.T, returned, preferred_element_type=jnp.float32)
        inner = jnp.mean(grad_norm * x_float, axis=-1, keepdims=True)
        grad_in = grad_float + scale * grad_norm - x_float * (scale * scale * scale) * inner
        return grad_in.astype(jnp.bfloat16), grad_mix

    last = section_count - 1
    early_step = min(1, last - 1)
    seed_float = cotangent.reshape(tokens, width).astype(jnp.float32)
    layer_in = inputs.reshape(tokens, width)
    outs = []
    saves = []
    grads_in = [None] * section_count
    mixes = [None] * section_count
    kepts = [None] * section_count
    for step in range(section_count):
        if step > 0:
            layer_in = hop(outs[-1], "section", step - 1, step)
        x_float = layer_in.astype(jnp.float32)
        scale = lax.rsqrt(jnp.mean(x_float * x_float, axis=-1, keepdims=True) + EPS)
        normed = (x_float * scale).astype(jnp.bfloat16)
        buffer = jnp.dot(tok_mat, normed, preferred_element_type=jnp.float32).astype(jnp.bfloat16)
        if step == early_step:
            buffer = jnp.where(section_index == last, grad_buffer(seed_float), buffer)
        received = to_experts(all_to_all(buffer, devices, width))
        if step == early_step:
            early_grad = received
        gate_pre, up_pre, hidden, results = expert_forward(received)
        if step == last:
            grad_back, grad_gate_pre, grad_up_pre = expert_backward(early_grad, gate_pre, up_pre)
            both = jnp.stack(
                [results.reshape(devices, -1, width), grad_back.reshape(devices, -1, width)], axis=1
            )
            back = lax.all_to_all(both, "expert", split_axis=0, concat_axis=0, tiled=True)
            returned = back[:, 0].reshape(-1, width)
            returned_grad = back[:, 1].reshape(-1, width)
            mixed, gathered = token_forward(x_float, returned)
            grads_in[step], mixes[step] = token_backward(
                seed_float, x_float, scale, gathered, returned_grad
            )
            kepts[step] = (received, early_grad, grad_gate_pre, grad_up_pre, hidden)
        else:
            returned = all_to_all(results.reshape(-1, width), devices, width)
            mixed, gathered = token_forward(x_float, returned)
        outs.append(mixed)
        saves.append((x_float, scale, received, gate_pre, up_pre, hidden, gathered))
    for step in reversed(range(last)):
        grad_out = hop(grads_in[step + 1], "section", step + 1, step)
        x_float, scale, received, gate_pre, up_pre, hidden, gathered = saves[step]
        grad_float = grad_out.astype(jnp.float32)
        grad_received = to_experts(all_to_all(grad_buffer(grad_float), devices, width))
        grad_back, grad_gate_pre, grad_up_pre = expert_backward(grad_received, gate_pre, up_pre)
        returned = all_to_all(grad_back.reshape(-1, width), devices, width)
        grads_in[step], mixes[step] = token_backward(grad_float, x_float, scale, gathered, returned)
        kepts[step] = (received, grad_received, grad_gate_pre, grad_up_pre, hidden)

    def pick(values):
        result = values[0]
        for step in range(1, section_count):
            result = jnp.where(section_index == step, values[step], result)
        return result

    def weight_grads(kept):
        received, grad_received, grad_gate_pre, grad_up_pre, hidden = kept
        grad_gate = jnp.einsum(
            "nemd,nemf->edf", received, grad_gate_pre, preferred_element_type=jnp.float32
        )
        grad_up = jnp.einsum("nemd,nemf->edf", received, grad_up_pre, preferred_element_type=jnp.float32)
        grad_down = jnp.einsum(
            "nemf,nemd->efd", hidden, grad_received, preferred_element_type=jnp.float32
        )
        return (
            grad_gate.astype(jnp.bfloat16),
            grad_up.astype(jnp.bfloat16),
            grad_down.astype(jnp.bfloat16),
        )

    branches = [lambda k=k: weight_grads(kepts[k]) for k in range(section_count)]
    grad_gate, grad_up, grad_down = lax.switch(section_index, branches)
    section_out = pick(outs).reshape(1, micro_count, tok_count, width)
    grad_input = pick(grads_in).reshape(1, micro_count, tok_count, width)
    grad_gates = pick(mixes).reshape(1, micro_count, tok_count, top_count)
    return (
        section_out,
        grad_input,
        grad_gates,
        grad_gate[None],
        grad_up[None],
        grad_down[None],
    )


def solution(mesh):
    in_specs = (
        P(None, "expert", None),
        P("section", None, "expert", None),
        P("section", None, "expert", None),
        P("section", "expert", None, None),
        P("section", "expert", None, None),
        P("section", "expert", None, None),
        P(None, "expert", None),
    )
    out_specs = (
        P("section", None, "expert", None),
        P("section", None, "expert", None),
        P("section", None, "expert", None),
        P("section", "expert", None, None),
        P("section", "expert", None, None),
        P("section", "expert", None, None),
    )
    return jax.shard_map(body, mesh=mesh, in_specs=in_specs, out_specs=out_specs, check_vma=False)
```

```python
import jax
import jax.numpy as jnp
from jax import lax
from jax.sharding import PartitionSpec as P

EPS = 1e-06


def hop(value, axis, source, target):
    return lax.ppermute(value, axis, [(source, target)])


def slot_matrices(ids, expert_count, most):
    micro_count, tok_count, top_count = ids.shape
    per_mb = tok_count * top_count
    flat = ids.reshape(micro_count, per_mb)
    order = jnp.arange(per_mb)
    earlier = order[:, None] > order[None, :]
    same = flat[:, :, None] == flat[:, None, :]
    position = jnp.sum(same & earlier[None], axis=2).astype(jnp.int32)
    micro = jnp.arange(micro_count, dtype=jnp.int32)[:, None]
    slot = flat * (micro_count * most) + micro * most + position
    slot = slot.reshape(-1)
    total_slots = expert_count * micro_count * most
    rows_mat = (jnp.arange(total_slots, dtype=jnp.int32)[:, None] == slot[None, :]).astype(jnp.bfloat16)
    tok_mat = rows_mat.reshape(total_slots, micro_count * tok_count, top_count).sum(axis=2)
    return rows_mat, tok_mat.astype(jnp.bfloat16)


def all_to_all(buffer, devices, width):
    shaped = buffer.reshape(devices, -1, width)
    out = lax.all_to_all(shaped, "expert", split_axis=0, concat_axis=0, tiled=True)
    return out.reshape(-1, width)


def body(inputs, route_ids, route_gates, w_gate, w_up, w_down, cotangent):
    section_count = lax.axis_size("section")
    section_index = lax.axis_index("section")
    devices = lax.axis_size("expert")
    micro_count, tok_count, width = inputs.shape
    top_count = route_ids.shape[3]
    exp_dev = w_gate.shape[1]
    hidden_width = w_gate.shape[3]
    expert_count = exp_dev * devices
    most = min(tok_count, 2 * tok_count * top_count // expert_count)
    slots_per = micro_count * most
    tokens = micro_count * tok_count
    gate_mat, up_mat, down_mat = (w_gate[0], w_up[0], w_down[0])
    ids = route_ids[0]
    gates = route_gates[0].reshape(tokens, top_count)
    rows_mat, tok_mat = slot_matrices(ids, expert_count, most)
    mix_mat = (rows_mat.T.astype(jnp.float32) * gates.reshape(-1)[:, None]).reshape(
        tokens, top_count, -1
    ).sum(axis=1)

    def to_experts(rows):
        return rows.reshape(devices, exp_dev, slots_per, -1)

    def expert_forward(received):
        gate_pre = jnp.einsum("nemd,edf->nemf", received, gate_mat, preferred_element_type=jnp.float32)
        up_pre = jnp.einsum("nemd,edf->nemf", received, up_mat, preferred_element_type=jnp.float32)
        hidden = (gate_pre * jax.nn.sigmoid(gate_pre) * up_pre).astype(jnp.bfloat16)
        results = jnp.einsum(
            "nemf,efd->nemd", hidden, down_mat, preferred_element_type=jnp.float32
        ).astype(jnp.bfloat16)
        return gate_pre, up_pre, hidden, results

    def hidden_grad(grad_received):
        return jnp.einsum("nemd,efd->nemf", grad_received, down_mat, preferred_element_type=jnp.float32)

    def expert_backward(grad_hidden, gate_pre, up_pre):
        sigma = jax.nn.sigmoid(gate_pre)
        active = gate_pre * sigma
        grad_gate_pre = (grad_hidden * up_pre * sigma * (1.0 + gate_pre * (1.0 - sigma))).astype(
            jnp.bfloat16
        )
        grad_up_pre = (grad_hidden * active).astype(jnp.bfloat16)
        grad_back = (
            jnp.einsum("nemf,edf->nemd", grad_gate_pre, gate_mat, preferred_element_type=jnp.float32)
            + jnp.einsum("nemf,edf->nemd", grad_up_pre, up_mat, preferred_element_type=jnp.float32)
        ).astype(jnp.bfloat16)
        return grad_back, grad_gate_pre, grad_up_pre

    def grad_buffer(grad_float):
        grad_rows = (gates[:, :, None] * grad_float[:, None, :]).astype(jnp.bfloat16).reshape(-1, width)
        return jnp.dot(rows_mat, grad_rows, preferred_element_type=jnp.float32).astype(jnp.bfloat16)

    def token_forward(x_float, returned):
        gathered = jnp.dot(rows_mat.T, returned, preferred_element_type=jnp.float32).astype(jnp.bfloat16)
        gathered = gathered.reshape(tokens, top_count, width)
        mixed = x_float + jnp.dot(
            mix_mat,
            returned.astype(jnp.float32),
            precision=lax.Precision.HIGHEST,
            preferred_element_type=jnp.float32,
        )
        return mixed.astype(jnp.bfloat16), gathered

    def token_backward(grad_float, x_float, scale, gathered, returned):
        grad_mix = jnp.sum(grad_float[:, None, :] * gathered.astype(jnp.float32), axis=-1)
        grad_norm = jnp.dot(tok_mat.T, returned, preferred_element_type=jnp.float32)
        inner = jnp.mean(grad_norm * x_float, axis=-1, keepdims=True)
        grad_in = grad_float + scale * grad_norm - x_float * (scale * scale * scale) * inner
        return grad_in.astype(jnp.bfloat16), grad_mix

    last = section_count - 1
    early_step = min(1, last - 1)
    seed_float = cotangent.reshape(tokens, width).astype(jnp.float32)
    layer_in = inputs.reshape(tokens, width)
    outs = []
    saves = []
    grads_in = [None] * section_count
    mixes = [None] * section_count
    kepts = [None] * section_count
    for step in range(section_count):
        if step > 0:
            layer_in = hop(outs[-1], "section", step - 1, step)
        x_float = layer_in.astype(jnp.float32)
        scale = lax.rsqrt(jnp.mean(x_float * x_float, axis=-1, keepdims=True) + EPS)
        normed = (x_float * scale).astype(jnp.bfloat16)
        buffer = jnp.dot(tok_mat, normed, preferred_element_type=jnp.float32).astype(jnp.bfloat16)
        if step == early_step:
            buffer = jnp.where(section_index == last, grad_buffer(seed_float), buffer)
        received = to_experts(all_to_all(buffer, devices, width))
        if step == early_step:
            early_grad = received
        if step == last:
            early_hidden = lax.cond(
                section_index == last,
                hidden_grad,
                lambda g: jnp.zeros(g.shape[:3] + (hidden_width,), jnp.float32),
                early_grad,
            )
        gate_pre, up_pre, hidden, results = expert_forward(received)
        if step == last:
            grad_back, grad_gate_pre, grad_up_pre = expert_backward(early_hidden, gate_pre, up_pre)
            both = jnp.stack(
                [results.reshape(devices, -1, width), grad_back.reshape(devices, -1, width)], axis=1
            )
            back = lax.all_to_all(both, "expert", split_axis=0, concat_axis=0, tiled=True)
            returned = back[:, 0].reshape(-1, width)
            returned_grad = back[:, 1].reshape(-1, width)
            mixed, gathered = token_forward(x_float, returned)
            grads_in[step], mixes[step] = token_backward(
                seed_float, x_float, scale, gathered, returned_grad
            )
            kepts[step] = (received, early_grad, grad_gate_pre, grad_up_pre, hidden)
        else:
            returned = all_to_all(results.reshape(-1, width), devices, width)
            mixed, gathered = token_forward(x_float, returned)
        outs.append(mixed)
        saves.append((x_float, scale, received, gate_pre, up_pre, hidden, gathered))
    for step in reversed(range(last)):
        grad_out = hop(grads_in[step + 1], "section", step + 1, step)
        x_float, scale, received, gate_pre, up_pre, hidden, gathered = saves[step]
        grad_float = grad_out.astype(jnp.float32)
        grad_received = to_experts(all_to_all(grad_buffer(grad_float), devices, width))
        grad_back, grad_gate_pre, grad_up_pre = expert_backward(
            hidden_grad(grad_received), gate_pre, up_pre
        )
        returned = all_to_all(grad_back.reshape(-1, width), devices, width)
        grads_in[step], mixes[step] = token_backward(grad_float, x_float, scale, gathered, returned)
        kepts[step] = (received, grad_received, grad_gate_pre, grad_up_pre, hidden)

    def pick(values):
        result = values[0]
        for step in range(1, section_count):
            result = jnp.where(section_index == step, values[step], result)
        return result

    def weight_grads(kept):
        received, grad_received, grad_gate_pre, grad_up_pre, hidden = kept
        grad_gate = jnp.einsum(
            "nemd,nemf->edf", received, grad_gate_pre, preferred_element_type=jnp.float32
        )
        grad_up = jnp.einsum("nemd,nemf->edf", received, grad_up_pre, preferred_element_type=jnp.float32)
        grad_down = jnp.einsum(
            "nemf,nemd->efd", hidden, grad_received, preferred_element_type=jnp.float32
        )
        return (
            grad_gate.astype(jnp.bfloat16),
            grad_up.astype(jnp.bfloat16),
            grad_down.astype(jnp.bfloat16),
        )

    branches = [lambda k=k: weight_grads(kepts[k]) for k in range(section_count)]
    grad_gate, grad_up, grad_down = lax.switch(section_index, branches)
    section_out = pick(outs).reshape(1, micro_count, tok_count, width)
    grad_input = pick(grads_in).reshape(1, micro_count, tok_count, width)
    grad_gates = pick(mixes).reshape(1, micro_count, tok_count, top_count)
    return (
        section_out,
        grad_input,
        grad_gates,
        grad_gate[None],
        grad_up[None],
        grad_down[None],
    )


def solution(mesh):
    in_specs = (
        P(None, "expert", None),
        P("section", None, "expert", None),
        P("section", None, "expert", None),
        P("section", "expert", None, None),
        P("section", "expert", None, None),
        P("section", "expert", None, None),
        P(None, "expert", None),
    )
    out_specs = (
        P("section", None, "expert", None),
        P("section", None, "expert", None),
        P("section", None, "expert", None),
        P("section", "expert", None, None),
        P("section", "expert", None, None),
        P("section", "expert", None, None),
    )
    return jax.shard_map(body, mesh=mesh, in_specs=in_specs, out_specs=out_specs, check_vma=False)
```

```python
import jax
import jax.numpy as jnp
from jax import lax
from jax.sharding import PartitionSpec as P

EPS = 1e-06


def hop(value, axis, source, target):
    return lax.ppermute(value, axis, [(source, target)])


def slot_matrices(ids, expert_count, most):
    micro_count, tok_count, top_count = ids.shape
    per_mb = tok_count * top_count
    flat = ids.reshape(micro_count, per_mb)
    order = jnp.arange(per_mb)
    earlier = order[:, None] > order[None, :]
    same = flat[:, :, None] == flat[:, None, :]
    position = jnp.sum(same & earlier[None], axis=2).astype(jnp.int32)
    micro = jnp.arange(micro_count, dtype=jnp.int32)[:, None]
    slot = flat * (micro_count * most) + micro * most + position
    slot = slot.reshape(-1)
    total_slots = expert_count * micro_count * most
    rows_mat = (jnp.arange(total_slots, dtype=jnp.int32)[:, None] == slot[None, :]).astype(jnp.bfloat16)
    tok_mat = rows_mat.reshape(total_slots, micro_count * tok_count, top_count).sum(axis=2)
    return rows_mat, tok_mat.astype(jnp.bfloat16)


def all_to_all(buffer, devices, width):
    shaped = buffer.reshape(devices, -1, width)
    out = lax.all_to_all(shaped, "expert", split_axis=0, concat_axis=0, tiled=True)
    return out.reshape(-1, width)


def body(inputs, route_ids, route_gates, w_gate, w_up, w_down, cotangent):
    section_count = lax.axis_size("section")
    section_index = lax.axis_index("section")
    devices = lax.axis_size("expert")
    micro_count, tok_count, width = inputs.shape
    top_count = route_ids.shape[3]
    exp_dev = w_gate.shape[1]
    hidden_width = w_gate.shape[3]
    expert_count = exp_dev * devices
    most = min(tok_count, 2 * tok_count * top_count // expert_count)
    slots_per = micro_count * most
    tokens = micro_count * tok_count
    gate_mat, up_mat, down_mat = (w_gate[0], w_up[0], w_down[0])
    ids = route_ids[0]
    gates = route_gates[0].reshape(tokens, top_count)
    rows_mat, tok_mat = slot_matrices(ids, expert_count, most)
    mix_mat = (rows_mat.T.astype(jnp.float32) * gates.reshape(-1)[:, None]).reshape(
        tokens, top_count, -1
    ).sum(axis=1)

    def to_experts(rows):
        return rows.reshape(devices, exp_dev, slots_per, -1)

    def expert_forward(received):
        gate_pre = jnp.einsum("nemd,edf->nemf", received, gate_mat, preferred_element_type=jnp.float32)
        up_pre = jnp.einsum("nemd,edf->nemf", received, up_mat, preferred_element_type=jnp.float32)
        hidden = (gate_pre * jax.nn.sigmoid(gate_pre) * up_pre).astype(jnp.bfloat16)
        results = jnp.einsum(
            "nemf,efd->nemd", hidden, down_mat, preferred_element_type=jnp.float32
        ).astype(jnp.bfloat16)
        return gate_pre, up_pre, hidden, results

    def expert_backward(grad_received, gate_pre, up_pre):
        sigma = jax.nn.sigmoid(gate_pre)
        active = gate_pre * sigma
        grad_hidden = jnp.einsum(
            "nemd,efd->nemf", grad_received, down_mat, preferred_element_type=jnp.float32
        )
        grad_gate_pre = (grad_hidden * up_pre * sigma * (1.0 + gate_pre * (1.0 - sigma))).astype(
            jnp.bfloat16
        )
        grad_up_pre = (grad_hidden * active).astype(jnp.bfloat16)
        grad_back = (
            jnp.einsum("nemf,edf->nemd", grad_gate_pre, gate_mat, preferred_element_type=jnp.float32)
            + jnp.einsum("nemf,edf->nemd", grad_up_pre, up_mat, preferred_element_type=jnp.float32)
        ).astype(jnp.bfloat16)
        return grad_back, grad_gate_pre, grad_up_pre

    def grad_buffer(grad_float):
        grad_rows = (gates[:, :, None] * grad_float[:, None, :]).astype(jnp.bfloat16).reshape(-1, width)
        return jnp.dot(rows_mat, grad_rows, preferred_element_type=jnp.float32).astype(jnp.bfloat16)

    def token_forward(x_float, returned):
        gathered = jnp.dot(rows_mat.T, returned, preferred_element_type=jnp.float32).astype(jnp.bfloat16)
        gathered = gathered.reshape(tokens, top_count, width)
        mixed = x_float + jnp.dot(
            mix_mat,
            returned.astype(jnp.float32),
            precision=lax.Precision.HIGHEST,
            preferred_element_type=jnp.float32,
        )
        return mixed.astype(jnp.bfloat16), gathered

    def token_backward(grad_float, x_float, scale, gathered, returned):
        grad_mix = jnp.sum(grad_float[:, None, :] * gathered.astype(jnp.float32), axis=-1)
        grad_norm = jnp.dot(tok_mat.T, returned, preferred_element_type=jnp.float32)
        inner = jnp.mean(grad_norm * x_float, axis=-1, keepdims=True)
        grad_in = grad_float + scale * grad_norm - x_float * (scale * scale * scale) * inner
        return grad_in.astype(jnp.bfloat16), grad_mix

    last = section_count - 1
    early_step = min(1, last - 1)
    seed_float = cotangent.reshape(tokens, width).astype(jnp.float32)
    layer_in = inputs.reshape(tokens, width)
    outs = []
    saves = []
    grads_in = [None] * section_count
    mixes = [None] * section_count
    kepts = [None] * section_count
    for step in range(section_count):
        if step > 0:
            layer_in = hop(outs[-1], "section", step - 1, step)
        x_float = layer_in.astype(jnp.float32)
        scale = lax.rsqrt(jnp.mean(x_float * x_float, axis=-1, keepdims=True) + EPS)
        normed = (x_float * scale).astype(jnp.bfloat16)
        buffer = jnp.dot(tok_mat, normed, preferred_element_type=jnp.float32).astype(jnp.bfloat16)
        if step == early_step:
            buffer = jnp.where(section_index == last, grad_buffer(seed_float), buffer)
        received = to_experts(all_to_all(buffer, devices, width))
        if step == early_step:
            early_grad = received
        gate_pre, up_pre, hidden, results = expert_forward(received)
        if step == last:
            grad_back, grad_gate_pre, grad_up_pre = expert_backward(early_grad, gate_pre, up_pre)
            both = jnp.concatenate(
                [results.reshape(devices, -1, width), grad_back.reshape(devices, -1, width)], axis=1
            )
            back = lax.all_to_all(both, "expert", split_axis=0, concat_axis=0, tiled=True)
            returned = back[:, :slots_per].reshape(-1, width)
            returned_grad = back[:, slots_per:].reshape(-1, width)
            mixed, gathered = token_forward(x_float, returned)
            grads_in[step], mixes[step] = token_backward(
                seed_float, x_float, scale, gathered, returned_grad
            )
            kepts[step] = (received, early_grad, grad_gate_pre, grad_up_pre, hidden)
        else:
            returned = all_to_all(results.reshape(-1, width), devices, width)
            mixed, gathered = token_forward(x_float, returned)
        outs.append(mixed)
        saves.append((x_float, scale, received, gate_pre, up_pre, hidden, gathered))
    for step in reversed(range(last)):
        grad_out = hop(grads_in[step + 1], "section", step + 1, step)
        x_float, scale, received, gate_pre, up_pre, hidden, gathered = saves[step]
        grad_float = grad_out.astype(jnp.float32)
        grad_received = to_experts(all_to_all(grad_buffer(grad_float), devices, width))
        grad_back, grad_gate_pre, grad_up_pre = expert_backward(grad_received, gate_pre, up_pre)
        returned = all_to_all(grad_back.reshape(-1, width), devices, width)
        grads_in[step], mixes[step] = token_backward(grad_float, x_float, scale, gathered, returned)
        kepts[step] = (received, grad_received, grad_gate_pre, grad_up_pre, hidden)

    def pick(values):
        result = values[0]
        for step in range(1, section_count):
            result = jnp.where(section_index == step, values[step], result)
        return result

    def weight_grads(kept):
        received, grad_received, grad_gate_pre, grad_up_pre, hidden = kept
        grad_gate = jnp.einsum(
            "nemd,nemf->edf", received, grad_gate_pre, preferred_element_type=jnp.float32
        )
        grad_up = jnp.einsum("nemd,nemf->edf", received, grad_up_pre, preferred_element_type=jnp.float32)
        grad_down = jnp.einsum(
            "nemf,nemd->efd", hidden, grad_received, preferred_element_type=jnp.float32
        )
        return (
            grad_gate.astype(jnp.bfloat16),
            grad_up.astype(jnp.bfloat16),
            grad_down.astype(jnp.bfloat16),
        )

    branches = [lambda k=k: weight_grads(kepts[k]) for k in range(section_count)]
    grad_gate, grad_up, grad_down = lax.switch(section_index, branches)
    section_out = pick(outs).reshape(1, micro_count, tok_count, width)
    grad_input = pick(grads_in).reshape(1, micro_count, tok_count, width)
    grad_gates = pick(mixes).reshape(1, micro_count, tok_count, top_count)
    return (
        section_out,
        grad_input,
        grad_gates,
        grad_gate[None],
        grad_up[None],
        grad_down[None],
    )


def solution(mesh):
    in_specs = (
        P(None, "expert", None),
        P("section", None, "expert", None),
        P("section", None, "expert", None),
        P("section", "expert", None, None),
        P("section", "expert", None, None),
        P("section", "expert", None, None),
        P(None, "expert", None),
    )
    out_specs = (
        P("section", None, "expert", None),
        P("section", None, "expert", None),
        P("section", None, "expert", None),
        P("section", "expert", None, None),
        P("section", "expert", None, None),
        P("section", "expert", None, None),
    )
    return jax.shard_map(body, mesh=mesh, in_specs=in_specs, out_specs=out_specs, check_vma=False)
```

```python
import jax
import jax.numpy as jnp
from jax import lax
from jax.sharding import PartitionSpec as P

EPS = 1e-06


def hop(value, axis, source, target):
    return lax.ppermute(value, axis, [(source, target)])


def slot_matrices(ids, expert_count, most):
    micro_count, tok_count, top_count = ids.shape
    per_mb = tok_count * top_count
    flat = ids.reshape(micro_count, per_mb)
    order = jnp.arange(per_mb)
    earlier = order[:, None] > order[None, :]
    same = flat[:, :, None] == flat[:, None, :]
    position = jnp.sum(same & earlier[None], axis=2).astype(jnp.int32)
    micro = jnp.arange(micro_count, dtype=jnp.int32)[:, None]
    slot = flat * (micro_count * most) + micro * most + position
    slot = slot.reshape(-1)
    total_slots = expert_count * micro_count * most
    rows_mat = (jnp.arange(total_slots, dtype=jnp.int32)[:, None] == slot[None, :]).astype(jnp.bfloat16)
    tok_mat = rows_mat.reshape(total_slots, micro_count * tok_count, top_count).sum(axis=2)
    return rows_mat, tok_mat.astype(jnp.bfloat16)


def all_to_all(buffer, devices, width):
    shaped = buffer.reshape(devices, -1, width)
    out = lax.all_to_all(shaped, "expert", split_axis=0, concat_axis=0, tiled=True)
    return out.reshape(-1, width)


def body(inputs, route_ids, route_gates, w_gate, w_up, w_down, cotangent):
    section_count = lax.axis_size("section")
    section_index = lax.axis_index("section")
    devices = lax.axis_size("expert")
    micro_count, tok_count, width = inputs.shape
    top_count = route_ids.shape[3]
    exp_dev = w_gate.shape[1]
    hidden_width = w_gate.shape[3]
    expert_count = exp_dev * devices
    most = min(tok_count, 2 * tok_count * top_count // expert_count)
    slots_per = micro_count * most
    tokens = micro_count * tok_count
    gate_mat, up_mat, down_mat = (w_gate[0], w_up[0], w_down[0])
    ids = route_ids[0]
    gates = route_gates[0].reshape(tokens, top_count)
    rows_mat, tok_mat = slot_matrices(ids, expert_count, most)
    mix_mat = (rows_mat.T.astype(jnp.float32) * gates.reshape(-1)[:, None]).reshape(
        tokens, top_count, -1
    ).sum(axis=1)

    def to_experts(rows):
        return rows.reshape(devices, exp_dev, slots_per, -1)

    def expert_forward(received):
        gate_pre = jnp.einsum("nemd,edf->nemf", received, gate_mat, preferred_element_type=jnp.float32)
        up_pre = jnp.einsum("nemd,edf->nemf", received, up_mat, preferred_element_type=jnp.float32)
        hidden = (gate_pre * jax.nn.sigmoid(gate_pre) * up_pre).astype(jnp.bfloat16)
        results = jnp.einsum(
            "nemf,efd->nemd", hidden, down_mat, preferred_element_type=jnp.float32
        ).astype(jnp.bfloat16)
        return gate_pre, up_pre, hidden, results

    def expert_backward(grad_received, gate_pre, up_pre):
        sigma = jax.nn.sigmoid(gate_pre)
        active = gate_pre * sigma
        grad_hidden = jnp.einsum(
            "nemd,efd->nemf", grad_received, down_mat, preferred_element_type=jnp.float32
        )
        grad_gate_pre = (grad_hidden * up_pre * sigma * (1.0 + gate_pre * (1.0 - sigma))).astype(
            jnp.bfloat16
        )
        grad_up_pre = (grad_hidden * active).astype(jnp.bfloat16)
        grad_back = (
            jnp.einsum("nemf,edf->nemd", grad_gate_pre, gate_mat, preferred_element_type=jnp.float32)
            + jnp.einsum("nemf,edf->nemd", grad_up_pre, up_mat, preferred_element_type=jnp.float32)
        ).astype(jnp.bfloat16)
        return grad_back, grad_gate_pre, grad_up_pre

    def grad_buffer(grad_float):
        return jnp.dot(
            mix_mat.T,
            grad_float,
            precision=lax.Precision.HIGHEST,
            preferred_element_type=jnp.float32,
        ).astype(jnp.bfloat16)

    def token_forward(x_float, returned):
        gathered = jnp.dot(rows_mat.T, returned, preferred_element_type=jnp.float32).astype(jnp.bfloat16)
        gathered = gathered.reshape(tokens, top_count, width)
        mixed = x_float + jnp.dot(
            mix_mat,
            returned.astype(jnp.float32),
            precision=lax.Precision.HIGHEST,
            preferred_element_type=jnp.float32,
        )
        return mixed.astype(jnp.bfloat16), gathered

    def token_backward(grad_float, x_float, scale, gathered, returned):
        grad_mix = jnp.sum(grad_float[:, None, :] * gathered.astype(jnp.float32), axis=-1)
        grad_norm = jnp.dot(tok_mat.T, returned, preferred_element_type=jnp.float32)
        inner = jnp.mean(grad_norm * x_float, axis=-1, keepdims=True)
        grad_in = grad_float + scale * grad_norm - x_float * (scale * scale * scale) * inner
        return grad_in.astype(jnp.bfloat16), grad_mix

    last = section_count - 1
    early_step = min(1, last - 1)
    seed_float = cotangent.reshape(tokens, width).astype(jnp.float32)
    layer_in = inputs.reshape(tokens, width)
    outs = []
    saves = []
    grads_in = [None] * section_count
    mixes = [None] * section_count
    kepts = [None] * section_count
    for step in range(section_count):
        if step > 0:
            layer_in = hop(outs[-1], "section", step - 1, step)
        x_float = layer_in.astype(jnp.float32)
        scale = lax.rsqrt(jnp.mean(x_float * x_float, axis=-1, keepdims=True) + EPS)
        normed = (x_float * scale).astype(jnp.bfloat16)
        buffer = jnp.dot(tok_mat, normed, preferred_element_type=jnp.float32).astype(jnp.bfloat16)
        if step == early_step:
            buffer = jnp.where(section_index == last, grad_buffer(seed_float), buffer)
        received = to_experts(all_to_all(buffer, devices, width))
        if step == early_step:
            early_grad = received
        gate_pre, up_pre, hidden, results = expert_forward(received)
        if step == last:
            grad_back, grad_gate_pre, grad_up_pre = expert_backward(early_grad, gate_pre, up_pre)
            both = jnp.stack(
                [results.reshape(devices, -1, width), grad_back.reshape(devices, -1, width)], axis=1
            )
            back = lax.all_to_all(both, "expert", split_axis=0, concat_axis=0, tiled=True)
            returned = back[:, 0].reshape(-1, width)
            returned_grad = back[:, 1].reshape(-1, width)
            mixed, gathered = token_forward(x_float, returned)
            grads_in[step], mixes[step] = token_backward(
                seed_float, x_float, scale, gathered, returned_grad
            )
            kepts[step] = (received, early_grad, grad_gate_pre, grad_up_pre, hidden)
        else:
            returned = all_to_all(results.reshape(-1, width), devices, width)
            mixed, gathered = token_forward(x_float, returned)
        outs.append(mixed)
        saves.append((x_float, scale, received, gate_pre, up_pre, hidden, gathered))
    for step in reversed(range(last)):
        grad_out = hop(grads_in[step + 1], "section", step + 1, step)
        x_float, scale, received, gate_pre, up_pre, hidden, gathered = saves[step]
        grad_float = grad_out.astype(jnp.float32)
        grad_received = to_experts(all_to_all(grad_buffer(grad_float), devices, width))
        grad_back, grad_gate_pre, grad_up_pre = expert_backward(grad_received, gate_pre, up_pre)
        returned = all_to_all(grad_back.reshape(-1, width), devices, width)
        grads_in[step], mixes[step] = token_backward(grad_float, x_float, scale, gathered, returned)
        kepts[step] = (received, grad_received, grad_gate_pre, grad_up_pre, hidden)

    def pick(values):
        result = values[0]
        for step in range(1, section_count):
            result = jnp.where(section_index == step, values[step], result)
        return result

    def weight_grads(kept):
        received, grad_received, grad_gate_pre, grad_up_pre, hidden = kept
        grad_gate = jnp.einsum(
            "nemd,nemf->edf", received, grad_gate_pre, preferred_element_type=jnp.float32
        )
        grad_up = jnp.einsum("nemd,nemf->edf", received, grad_up_pre, preferred_element_type=jnp.float32)
        grad_down = jnp.einsum(
            "nemf,nemd->efd", hidden, grad_received, preferred_element_type=jnp.float32
        )
        return (
            grad_gate.astype(jnp.bfloat16),
            grad_up.astype(jnp.bfloat16),
            grad_down.astype(jnp.bfloat16),
        )

    branches = [lambda k=k: weight_grads(kepts[k]) for k in range(section_count)]
    grad_gate, grad_up, grad_down = lax.switch(section_index, branches)
    section_out = pick(outs).reshape(1, micro_count, tok_count, width)
    grad_input = pick(grads_in).reshape(1, micro_count, tok_count, width)
    grad_gates = pick(mixes).reshape(1, micro_count, tok_count, top_count)
    return (
        section_out,
        grad_input,
        grad_gates,
        grad_gate[None],
        grad_up[None],
        grad_down[None],
    )


def solution(mesh):
    in_specs = (
        P(None, "expert", None),
        P("section", None, "expert", None),
        P("section", None, "expert", None),
        P("section", "expert", None, None),
        P("section", "expert", None, None),
        P("section", "expert", None, None),
        P(None, "expert", None),
    )
    out_specs = (
        P("section", None, "expert", None),
        P("section", None, "expert", None),
        P("section", None, "expert", None),
        P("section", "expert", None, None),
        P("section", "expert", None, None),
        P("section", "expert", None, None),
    )
    return jax.shard_map(body, mesh=mesh, in_specs=in_specs, out_specs=out_specs, check_vma=False)
```
